256 devices in a mesh: seq: 64 (over z, y, core), tensor: 4 (over x).
Axes of the slice: x: 4, y: 4, z: 8, core: 2. Of those that a mesh axis runs over, the one named last changes fastest.
Arguments:
- new_states: bfloat16 [4, 128, 1024], P(None, None, 'tensor'), may hold values from -6 to 6
- self_query: bfloat16 [1024, 1024], P(None, 'tensor'), may hold values from -0.1875 to 0.1875
- self_key: bfloat16 [1024, 1024], P(None, 'tensor'), may hold values from -0.375 to 0.375
- self_value: bfloat16 [1024, 1024], P(None, 'tensor'), may hold values from -0.1875 to 0.1875
- self_output: bfloat16 [1024, 1024], P('tensor'), may hold values from -0.1875 to 0.1875
- cross_query: bfloat16 [1024, 1024], P(None, 'tensor'), may hold values from -0.1875 to 0.1875
- cross_output: bfloat16 [1024, 1024], P('tensor'), may hold values from -0.1875 to 0.1875
- feed_up: bfloat16 [1024, 4096], P(None, 'tensor'), may hold values from -0.1875 to 0.1875
- feed_down: bfloat16 [4096, 1024], P('tensor'), may hold values from -0.09375 to 0.09375
- norm_self: float32 [1024], replicated, may hold values from 0.25 to 1.75
- norm_cross: float32 [1024], replicated, may hold values from 0.25 to 1.75
- norm_feed: float32 [1024], replicated, may hold values from 0.25 to 1.75
- self_cache: bfloat16 [1536, 2, 128, 1024], P('seq', None, None, 'tensor'), may hold values from -240 to 240
- cross_cache: bfloat16 [128, 2, 512, 1024], P(None, None, 'seq', 'tensor'), may hold values from -240 to 240
- cache_lengths: int32 [128], replicated, may hold values from 1 to 16384, as said below
- page_table: int32 [128, 128], replicated, may hold values from -1 to 1535, as said below
- request_order: int32 [128], replicated, may hold values from 0 to 127, each once
- encoder_lengths: int32 [128], replicated, may hold values from 1 to 512, as said below
Outputs:
- out: bfloat16 [4, 128, 1024], P(None, None, 'tensor')
The draws below stay inside these ranges and needn't reach their ends.
Inputs may be any that keep to these rules, and one draw needn't show every extreme that they name: `cache_lengths`: one request has exactly 16384 cached tokens. `page_table`: row r holds the slots of request r's pages in order: its first ceil(cache_lengths[r] / 128) entries are slots, page p holding positions p * 128 to (p + 1) * 128 - 1, and no slot appears twice in the table; the other entries are -1. Slot s belongs to seq index s // 24. `encoder_lengths`: one request has exactly 512 encoder positions.
All inputs are finite; a program needn't handle non-finite values.
Results may differ from the reference program's by a relative error of at most 0.014.
The reference program's roundings to bfloat16 on the way (of `queries`, `self_attn`, `first_norm`, `cross_queries`, `cross_attn`, `second_norm` and `ffn_hidden`) count: a program that leaves them out, or rounds other values in their place, can miss the bound.
Values may be sent and summed in bfloat16 or wider, within the bound.
No kernel may reach another device: no remote copies, remote signals or barrier semaphores. Data moves between devices by JAX's collectives and lax.ppermute only.
A program may use at most 64 MiB of HBM per device.

```python
import jax
import jax.numpy as jnp
from jax import lax

D = 1024
HEADS = 16
HEAD_DIM = 64
FF = 4096
STEPS = 4
PAGE = 128
P_DEV = 24
ENC = 512
REQUESTS = 128
POOL = 1536
MAXP = 128


def page_plan(key):
    base = jax.random.fold_in(key, 11)
    key_weight, key_big, key_tail, key_device, key_full, key_order, key_assign = jax.random.split(base, 7)
    budget = POOL * 2 // 5 - MAXP
    raw_weight = jax.random.randint(key_weight, (REQUESTS,), 1, 65)
    page_count = jnp.maximum(1, raw_weight * budget // jnp.sum(raw_weight))
    page_count = jnp.minimum(page_count, MAXP)
    request_ids = jnp.arange(REQUESTS)
    longest = jax.random.randint(key_big, (), 0, REQUESTS)
    page_count = jnp.where(request_ids == longest, MAXP, page_count)
    tail_tokens = jax.random.randint(key_tail, (REQUESTS,), 1, PAGE + 1)
    lengths = jnp.where(request_ids == longest, MAXP * PAGE, (page_count - 1) * PAGE + tail_tokens)
    slot_ids = jnp.arange(POOL)
    device_of = slot_ids // P_DEV
    within = slot_ids % P_DEV
    device_weight = jax.random.randint(key_device, (POOL // P_DEV,), 1, 5)
    full_device = jax.random.randint(key_full, (), 0, POOL // P_DEV)
    priority = jnp.where(device_of == full_device, within - 12 * P_DEV, within * 12 // device_weight[device_of])
    priority = jnp.where(slot_ids == POOL - 1, -13 * P_DEV, priority)
    priority = priority * POOL + jax.random.permutation(key_order, POOL)
    slot_order = jnp.argsort(priority)
    page_total = jnp.sum(page_count)
    shuffle_score = jax.random.permutation(key_assign, POOL) + jnp.where(slot_ids < page_total, 0, POOL)
    used_order = slot_order[jnp.argsort(shuffle_score)]
    starts = jnp.cumsum(page_count) - page_count
    page_ids = jnp.arange(MAXP)
    entry = jnp.minimum(starts[:, None] + page_ids[None, :], POOL - 1)
    table = jnp.where(page_ids[None, :] < page_count[:, None], used_order[entry], -1)
    return (lengths.astype(jnp.int32), table.astype(jnp.int32))


def draw_cache_lengths(key, part):
    return page_plan(key)[0]


def draw_page_table(key, part):
    return page_plan(key)[1]


def attention_cache(key, shape):
    scale = jnp.array([2.0, 1.0], jnp.float32).reshape(1, 2, 1, 1)
    base = jnp.clip(jax.random.normal(key, shape, jnp.float32), -6.0, 6.0)
    return (base * scale).astype(jnp.bfloat16)


def draw_self_cache(key, part):
    return attention_cache(jax.random.fold_in(key, 21), (POOL, 2, PAGE, D))


def draw_cross_cache(key, part):
    return attention_cache(jax.random.fold_in(key, 22), (REQUESTS, 2, ENC, D))


def draw_encoder_lengths(key, part):
    key_len, key_big = jax.random.split(jax.random.fold_in(key, 5))
    lengths = jax.random.randint(key_len, (REQUESTS,), 1, ENC + 1)
    longest = jax.random.randint(key_big, (), 0, REQUESTS)
    return jnp.where(jnp.arange(REQUESTS) == longest, ENC, lengths).astype(jnp.int32)


def levels(own_key, dims, pieces, smallest, top_value):
    loudness = 1.0
    for position, blocks in pieces:
        steps = jax.random.uniform(jax.random.fold_in(jax.random.fold_in(own_key, 6), position), (blocks,), jnp.float32, smallest / len(pieces), top_value / len(pieces))
        loudness = loudness * jnp.repeat(jnp.exp(steps), dims[position] // blocks).reshape((-1,) + (1,) * (len(dims) - 1 - position))
    return loudness


def centred(own_key, dims, deviation, limit, pieces=(), held_as=jnp.bfloat16):
    values = jax.random.normal(own_key, dims, jnp.float32) * deviation
    if len(pieces) > 0:
        values = levels(own_key, dims, pieces, -0.22, 0.18) * values
    return jnp.clip(values, min=-limit, max=limit).astype(held_as)


def setup_inputs(seed: int = 0) -> dict:
    seeds = jax.random.split(jax.random.key(seed), 19)
    return {
        "new_states": centred(seeds[0], (STEPS, REQUESTS, D), 1.0, 6.0, ((2, 4),)),
        "self_query": centred(seeds[1], (D, D), D ** -0.5, 0.1875, ((1, 4),)),
        "self_key": centred(seeds[2], (D, D), (D // 4) ** -0.5, 0.375, ((1, 4),)),
        "self_value": centred(seeds[3], (D, D), D ** -0.5, 0.1875, ((1, 4),)),
        "self_output": centred(seeds[4], (D, D), D ** -0.5, 0.1875, ((0, 4),)),
        "cross_query": centred(seeds[5], (D, D), D ** -0.5, 0.1875, ((1, 4),)),
        "cross_output": centred(seeds[6], (D, D), D ** -0.5, 0.1875, ((0, 4),)),
        "feed_up": centred(seeds[7], (D, FF), D ** -0.5, 0.1875, ((1, 4),)),
        "feed_down": centred(seeds[8], (FF, D), FF ** -0.5, 0.09375, ((0, 4),)),
        "norm_self": jnp.clip(1.0 + 0.15 * jax.random.normal(seeds[9], (D,), jnp.float32), 0.25, 1.75),
        "norm_cross": jnp.clip(1.0 + 0.15 * jax.random.normal(seeds[10], (D,), jnp.float32), 0.25, 1.75),
        "norm_feed": jnp.clip(1.0 + 0.15 * jax.random.normal(seeds[11], (D,), jnp.float32), 0.25, 1.75),
        "self_cache": draw_self_cache(jax.random.fold_in(seeds[18], 71), 0),
        "cross_cache": draw_cross_cache(jax.random.fold_in(seeds[18], 71), 0),
        "cache_lengths": draw_cache_lengths(jax.random.fold_in(seeds[18], 71), 0),
        "page_table": draw_page_table(jax.random.fold_in(seeds[18], 71), 0),
        "request_order": jax.random.permutation(seeds[16], REQUESTS).astype(jnp.int32),
        "encoder_lengths": draw_encoder_lengths(jax.random.fold_in(seeds[18], 71), 0),
    }


EPSILON = 1e-05
NEG_FILL = -1e+30

def layer_norm(summed, gain):
    center = lax.optimization_barrier(jnp.mean(summed, axis=-1, keepdims=True))
    spread = lax.optimization_barrier(jnp.mean(summed * summed, axis=-1, keepdims=True)) - center * center
    return (summed - center) * lax.rsqrt(spread + EPSILON) * gain.astype(jnp.float32)

def rounded_weights(weights):
    return lax.optimization_barrier(weights.astype(jnp.bfloat16)).astype(jnp.float32)

def head_grid(flat):
    return jnp.transpose(flat.reshape(STEPS, REQUESTS, HEADS, HEAD_DIM), (1, 0, 2, 3))

def reference(new_states, self_query, self_key, self_value, self_output, cross_query, cross_output, feed_up, feed_down, norm_self, norm_cross, norm_feed, self_cache, cross_cache, cache_lengths, page_table, request_order, encoder_lengths):
    scaling = HEAD_DIM ** (-0.5)
    flat = new_states.reshape(STEPS * REQUESTS, D)
    queries = (jnp.dot(flat, self_query, preferred_element_type=jnp.float32) * scaling).astype(jnp.bfloat16)
    new_keys = jnp.dot(flat, self_key, preferred_element_type=jnp.float32).astype(jnp.bfloat16)
    new_values = jnp.dot(flat, self_value, preferred_element_type=jnp.float32).astype(jnp.bfloat16)
    causal = (jnp.arange(STEPS)[None, :] <= jnp.arange(STEPS)[:, None])[:, None, :]

    def self_row(items):
        query_row, key_row, value_row, request = items
        pages = jnp.maximum(page_table[request], 0)
        gathered = self_cache[pages]
        cache_keys = gathered[:, 0].reshape(MAXP * PAGE, HEADS, HEAD_DIM).astype(jnp.float32)
        cache_values = gathered[:, 1].reshape(MAXP * PAGE, HEADS, HEAD_DIM).astype(jnp.float32)
        allowed = (jnp.arange(MAXP * PAGE) < cache_lengths[request])[None, None, :]
        query_wide = query_row.astype(jnp.float32)
        cache_scores = jnp.where(allowed, jnp.einsum('thd,khd->thk', query_wide, cache_keys), NEG_FILL)
        new_scores = jnp.where(causal, jnp.einsum('thd,uhd->thu', query_wide, key_row.astype(jnp.float32)), NEG_FILL)
        top = jnp.maximum(lax.optimization_barrier(jnp.max(cache_scores, axis=-1)), lax.optimization_barrier(jnp.max(new_scores, axis=-1)))[..., None]
        cache_weights = jnp.where(allowed, jnp.exp(cache_scores - top), 0.0)
        new_weights = jnp.where(causal, jnp.exp(new_scores - top), 0.0)
        denom = lax.optimization_barrier(jnp.sum(cache_weights, axis=-1)) + lax.optimization_barrier(jnp.sum(new_weights, axis=-1))
        numer = jnp.einsum('thk,khd->thd', rounded_weights(cache_weights), cache_values)
        numer = numer + jnp.einsum('thu,uhd->thd', rounded_weights(new_weights), value_row.astype(jnp.float32))
        return (numer / denom[..., None]).reshape(STEPS, D).astype(jnp.bfloat16)
    self_attn = lax.map(self_row, (head_grid(queries), head_grid(new_keys), head_grid(new_values), request_order))
    self_attn = jnp.transpose(self_attn, (1, 0, 2)).reshape(STEPS * REQUESTS, D)
    first_norm = layer_norm(flat.astype(jnp.float32) + jnp.dot(self_attn, self_output, preferred_element_type=jnp.float32), norm_self).astype(jnp.bfloat16)
    cross_queries = (jnp.dot(first_norm, cross_query, preferred_element_type=jnp.float32) * scaling).astype(jnp.bfloat16)

    def cross_row(items):
        query_row, request = items
        encoded = cross_cache[request]
        enc_keys = encoded[0].reshape(ENC, HEADS, HEAD_DIM).astype(jnp.float32)
        enc_values = encoded[1].reshape(ENC, HEADS, HEAD_DIM).astype(jnp.float32)
        allowed = (jnp.arange(ENC) < encoder_lengths[request])[None, None, :]
        scores = jnp.where(allowed, jnp.einsum('thd,ehd->the', query_row.astype(jnp.float32), enc_keys), NEG_FILL)
        top = lax.optimization_barrier(jnp.max(scores, axis=-1, keepdims=True))
        weights = jnp.where(allowed, jnp.exp(scores - top), 0.0)
        denom = lax.optimization_barrier(jnp.sum(weights, axis=-1))
        numer = jnp.einsum('the,ehd->thd', rounded_weights(weights), enc_values)
        return (numer / denom[..., None]).reshape(STEPS, D).astype(jnp.bfloat16)
    cross_attn = lax.map(cross_row, (head_grid(cross_queries), request_order))
    cross_attn = jnp.transpose(cross_attn, (1, 0, 2)).reshape(STEPS * REQUESTS, D)
    second_norm = layer_norm(first_norm.astype(jnp.float32) + jnp.dot(cross_attn, cross_output, preferred_element_type=jnp.float32), norm_cross).astype(jnp.bfloat16)
    ffn_hidden = jax.nn.gelu(jnp.dot(second_norm, feed_up, preferred_element_type=jnp.float32), approximate=False).astype(jnp.bfloat16)
    summed = second_norm.astype(jnp.float32) + jnp.dot(ffn_hidden, feed_down, preferred_element_type=jnp.float32)
    return layer_norm(summed, norm_feed).astype(jnp.bfloat16).reshape(STEPS, REQUESTS, D)
```

```python
import jax
import jax.numpy as jnp
from jax import lax
from jax.sharding import PartitionSpec as P

HEAD_DIM = 64


EPSILON = 1e-05
NEG_FILL = -1e30


def layer_norm(summed, gain):
    center = jnp.mean(summed, axis=-1, keepdims=True)
    spread = jnp.mean(summed * summed, axis=-1, keepdims=True) - center * center
    return (summed - center) * lax.rsqrt(spread + EPSILON) * gain


def global_max(local_max, size):
    result = local_max
    distance = 1
    while distance < size:
        pairs = [(i, i ^ distance) for i in range(size)]
        result = jnp.maximum(result, lax.ppermute(result, "seq", pairs))
        distance *= 2
    return result


def global_totals(denom, numer):
    packed = jnp.concatenate([numer.reshape(-1), denom.reshape(-1)])
    packed = lax.psum(packed, "seq")
    count = numer.size
    return (packed[count:].reshape(denom.shape), packed[:count].reshape(numer.shape))


def reduce_norm(residual, partial_value, gain):
    width = residual.shape[1]
    total = lax.psum(partial_value, "tensor")
    full = layer_norm(residual.astype(jnp.float32) + total, gain).astype(jnp.bfloat16)
    columns = width // lax.axis_size("tensor")
    return (full, lax.dynamic_slice_in_dim(full, lax.axis_index("tensor") * columns, columns, 1))


def on_device(
    new_states,
    self_query,
    self_key,
    self_value,
    self_output,
    cross_query,
    cross_output,
    feed_up,
    feed_down,
    norm_self,
    norm_cross,
    norm_feed,
    self_cache,
    cross_cache,
    cache_lengths,
    page_table,
    request_order,
    encoder_lengths,
):
    states = lax.all_gather(new_states, "tensor", axis=2, tiled=True)
    steps, requests, width = states.shape
    flat = states.reshape(steps * requests, width)
    local_width = self_query.shape[1]
    local_heads = local_width // HEAD_DIM
    scaling = HEAD_DIM ** (-0.5)
    queries = (jnp.dot(flat, self_query, preferred_element_type=jnp.float32) * scaling).astype(
        jnp.bfloat16
    )
    new_keys = jnp.dot(flat, self_key, preferred_element_type=jnp.float32).astype(jnp.bfloat16)
    new_values = jnp.dot(flat, self_value, preferred_element_type=jnp.float32).astype(jnp.bfloat16)
    query_grid = queries.reshape(steps, requests, local_heads, HEAD_DIM)
    key_grid = new_keys.reshape(steps, requests, local_heads, HEAD_DIM)
    value_grid = new_values.reshape(steps, requests, local_heads, HEAD_DIM)
    slot_count = self_cache.shape[0]
    page_width = self_cache.shape[2]
    max_pages = page_table.shape[1]
    seq_index = lax.axis_index("seq")
    seq_size = lax.axis_size("seq")
    flat_table = page_table.reshape(-1)
    entry_ids = jnp.arange(requests * max_pages, dtype=jnp.int32)
    entry_request = entry_ids // max_pages
    entry_page = entry_ids % max_pages
    slot_ids = seq_index * slot_count + jnp.arange(slot_count, dtype=jnp.int32)
    matches = flat_table[None, :] == slot_ids[:, None]
    slot_live = jnp.any(matches, axis=1)
    slot_owner = jnp.sum(jnp.where(matches, entry_request[None, :], 0), axis=1)
    slot_page = jnp.sum(jnp.where(matches, entry_page[None, :], 0), axis=1)
    request_ids = jnp.arange(requests, dtype=jnp.int32)
    slot_length = jnp.sum(
        jnp.where(slot_owner[:, None] == request_ids[None, :], cache_lengths[None, :], 0), axis=1
    )
    positions = slot_page[:, None] * page_width + jnp.arange(page_width, dtype=jnp.int32)[None, :]
    slot_valid = slot_live[:, None] & (positions < slot_length[:, None])
    slot_rows = slot_live[:, None] & (request_order[None, :] == slot_owner[:, None])
    rows_half = slot_rows.astype(jnp.bfloat16)
    rows_wide = slot_rows.astype(jnp.float32)
    slot_query = jnp.einsum(
        "pb,sbc->psc",
        rows_half,
        queries.reshape(steps, requests, local_width),
        preferred_element_type=jnp.float32,
    ).astype(jnp.bfloat16)
    slot_query = slot_query.reshape(slot_count, steps, local_heads, HEAD_DIM)
    cache_keys = self_cache[:, 0].reshape(slot_count, page_width, local_heads, HEAD_DIM)
    cache_values = self_cache[:, 1].reshape(slot_count, page_width, local_heads, HEAD_DIM)
    cache_scores = jnp.einsum(
        "pshd,pkhd->pshk", slot_query, cache_keys, preferred_element_type=jnp.float32
    )
    valid_grid = slot_valid[:, None, None, :]
    slot_max = jnp.max(jnp.where(valid_grid, cache_scores, NEG_FILL), axis=3)
    row_max = jnp.max(
        jnp.where(slot_rows[:, None, :, None], slot_max[:, :, None, :], NEG_FILL), axis=0
    )
    causal = jnp.arange(steps)[None, :] <= jnp.arange(steps)[:, None]
    new_scores = jnp.einsum(
        "tbhd,ubhd->bhtu", query_grid, key_grid, preferred_element_type=jnp.float32
    )
    new_scores = jnp.where(causal, new_scores, NEG_FILL)
    new_max = jnp.transpose(jnp.max(new_scores, axis=3), (2, 0, 1))
    top = global_max(jnp.maximum(row_max, new_max), seq_size)
    slot_top = jnp.einsum("pb,sbh->psh", rows_wide, top, precision=lax.Precision.HIGHEST)
    cache_weights = jnp.exp(jnp.where(valid_grid, cache_scores - slot_top[..., None], NEG_FILL))
    cache_denom = jnp.sum(cache_weights, axis=3)
    cache_numer = jnp.einsum(
        "pshk,pkhd->pshd",
        cache_weights.astype(jnp.bfloat16),
        cache_values,
        preferred_element_type=jnp.float32,
    )
    row_denom = jnp.einsum("pb,psh->sbh", rows_wide, cache_denom, precision=lax.Precision.HIGHEST)
    row_numer = jnp.einsum("pb,pshd->sbhd", rows_wide, cache_numer, precision=lax.Precision.HIGHEST)
    total_denom, total_numer = global_totals(row_denom, row_numer)
    top_new = jnp.transpose(top, (1, 2, 0))[..., None]
    new_weights = jnp.where(causal, jnp.exp(new_scores - top_new), 0.0)
    new_denom = jnp.transpose(jnp.sum(new_weights, axis=3), (2, 0, 1))
    new_numer = jnp.einsum(
        "bhtu,ubhd->tbhd",
        new_weights.astype(jnp.bfloat16),
        value_grid,
        preferred_element_type=jnp.float32,
    )
    self_attn = ((total_numer + new_numer) / (total_denom + new_denom)[..., None]).astype(
        jnp.bfloat16
    )
    partial_value = jnp.dot(
        self_attn.reshape(steps * requests, local_width),
        self_output,
        preferred_element_type=jnp.float32,
    )
    first_full, first_share = reduce_norm(flat, partial_value, norm_self)
    cross_queries = (
        jnp.dot(first_full, cross_query, preferred_element_type=jnp.float32) * scaling
    ).astype(jnp.bfloat16)
    cross_grid = cross_queries.reshape(steps, requests, local_heads, HEAD_DIM)
    order_rows = (request_order[:, None] == request_ids[None, :]).astype(jnp.bfloat16)
    request_query = jnp.einsum(
        "br,sbhd->srhd", order_rows, cross_grid, preferred_element_type=jnp.float32
    ).astype(jnp.bfloat16)
    enc_local = cross_cache.shape[2]
    enc_keys = cross_cache[:, 0].reshape(requests, enc_local, local_heads, HEAD_DIM)
    enc_values = cross_cache[:, 1].reshape(requests, enc_local, local_heads, HEAD_DIM)
    enc_positions = seq_index * enc_local + jnp.arange(enc_local, dtype=jnp.int32)
    enc_valid = (enc_positions[None, :] < encoder_lengths[:, None])[None, :, None, :]
    enc_scores = jnp.einsum(
        "srhd,rehd->srhe", request_query, enc_keys, preferred_element_type=jnp.float32
    )
    enc_top = global_max(jnp.max(jnp.where(enc_valid, enc_scores, NEG_FILL), axis=3), seq_size)
    enc_weights = jnp.exp(jnp.where(enc_valid, enc_scores - enc_top[..., None], NEG_FILL))
    enc_numer_local = jnp.einsum(
        "srhe,rehd->srhd",
        enc_weights.astype(jnp.bfloat16),
        enc_values,
        preferred_element_type=jnp.float32,
    )
    enc_denom, enc_numer = global_totals(jnp.sum(enc_weights, axis=3), enc_numer_local)
    enc_attn = (enc_numer / enc_denom[..., None]).astype(jnp.bfloat16)
    cross_attn = jnp.einsum(
        "br,srhd->sbhd", order_rows, enc_attn, preferred_element_type=jnp.float32
    ).astype(jnp.bfloat16)
    partial_value = jnp.dot(
        cross_attn.reshape(steps * requests, local_width),
        cross_output,
        preferred_element_type=jnp.float32,
    )
    second_full, second_share = reduce_norm(first_full, partial_value, norm_cross)
    ffn_hidden = jax.nn.gelu(
        jnp.dot(second_full, feed_up, preferred_element_type=jnp.float32), approximate=False
    ).astype(jnp.bfloat16)
    ignored, out_share = reduce_norm(
        second_full, jnp.dot(ffn_hidden, feed_down, preferred_element_type=jnp.float32), norm_feed
    )
    return out_share.reshape(steps, requests, out_share.shape[1])


def solution(mesh):
    in_specs = (
        P(None, None, "tensor"),
        P(None, "tensor"),
        P(None, "tensor"),
        P(None, "tensor"),
        P("tensor", None),
        P(None, "tensor"),
        P("tensor", None),
        P(None, "tensor"),
        P("tensor", None),
        P(),
        P(),
        P(),
        P("seq", None, None, "tensor"),
        P(None, None, "seq", "tensor"),
        P(),
        P(),
        P(),
        P(),
    )
    out_specs = P(None, None, "tensor")
    return jax.shard_map(
        on_device, mesh=mesh, in_specs=in_specs, out_specs=out_specs, check_vma=False
    )
```

```python
import jax
import jax.numpy as jnp
from jax import lax
from jax.sharding import PartitionSpec as P

HEAD_DIM = 64


EPSILON = 1e-05
NEG_FILL = -1e30


def layer_norm(summed, gain):
    center = jnp.mean(summed, axis=-1, keepdims=True)
    spread = jnp.mean(summed * summed, axis=-1, keepdims=True) - center * center
    return (summed - center) * lax.rsqrt(spread + EPSILON) * gain


def combine_seq(top, denom, numer, size):
    index = lax.axis_index("seq")
    distance = 1
    while distance < size:
        pairs = [(i, i ^ distance) for i in range(size)]
        other_top, other_denom, other_numer = lax.ppermute((top, denom, numer), "seq", pairs)
        low = (index & distance) == 0
        top_a = jnp.where(low, top, other_top)
        top_b = jnp.where(low, other_top, top)
        denom_a = jnp.where(low, denom, other_denom)
        denom_b = jnp.where(low, other_denom, denom)
        numer_a = jnp.where(low, numer, other_numer)
        numer_b = jnp.where(low, other_numer, numer)
        merged = jnp.maximum(top_a, top_b)
        scale_a = jnp.exp(top_a - merged)
        scale_b = jnp.exp(top_b - merged)
        denom = denom_a * scale_a + denom_b * scale_b
        numer = numer_a * scale_a[..., None] + numer_b * scale_b[..., None]
        top = merged
        distance *= 2
    return top, denom, numer


def reduce_norm(residual, partial_value, gain):
    width = residual.shape[1]
    total = lax.psum(partial_value, "tensor")
    full = layer_norm(residual.astype(jnp.float32) + total, gain).astype(jnp.bfloat16)
    columns = width // lax.axis_size("tensor")
    return (full, lax.dynamic_slice_in_dim(full, lax.axis_index("tensor") * columns, columns, 1))


def on_device(
    new_states,
    self_query,
    self_key,
    self_value,
    self_output,
    cross_query,
    cross_output,
    feed_up,
    feed_down,
    norm_self,
    norm_cross,
    norm_feed,
    self_cache,
    cross_cache,
    cache_lengths,
    page_table,
    request_order,
    encoder_lengths,
):
    states = lax.all_gather(new_states, "tensor", axis=2, tiled=True)
    steps, requests, width = states.shape
    flat = states.reshape(steps * requests, width)
    local_width = self_query.shape[1]
    local_heads = local_width // HEAD_DIM
    scaling = HEAD_DIM ** (-0.5)
    queries = (jnp.dot(flat, self_query, preferred_element_type=jnp.float32) * scaling).astype(
        jnp.bfloat16
    )
    new_keys = jnp.dot(flat, self_key, preferred_element_type=jnp.float32).astype(jnp.bfloat16)
    new_values = jnp.dot(flat, self_value, preferred_element_type=jnp.float32).astype(jnp.bfloat16)
    query_grid = queries.reshape(steps, requests, local_heads, HEAD_DIM)
    key_grid = new_keys.reshape(steps, requests, local_heads, HEAD_DIM)
    value_grid = new_values.reshape(steps, requests, local_heads, HEAD_DIM)
    slot_count = self_cache.shape[0]
    page_width = self_cache.shape[2]
    max_pages = page_table.shape[1]
    seq_index = lax.axis_index("seq")
    seq_size = lax.axis_size("seq")
    flat_table = page_table.reshape(-1)
    entry_ids = jnp.arange(requests * max_pages, dtype=jnp.int32)
    entry_request = entry_ids // max_pages
    entry_page = entry_ids % max_pages
    slot_ids = seq_index * slot_count + jnp.arange(slot_count, dtype=jnp.int32)
    matches = flat_table[None, :] == slot_ids[:, None]
    slot_live = jnp.any(matches, axis=1)
    slot_owner = jnp.sum(jnp.where(matches, entry_request[None, :], 0), axis=1)
    slot_page = jnp.sum(jnp.where(matches, entry_page[None, :], 0), axis=1)
    request_ids = jnp.arange(requests, dtype=jnp.int32)
    slot_length = jnp.sum(
        jnp.where(slot_owner[:, None] == request_ids[None, :], cache_lengths[None, :], 0), axis=1
    )
    positions = slot_page[:, None] * page_width + jnp.arange(page_width, dtype=jnp.int32)[None, :]
    slot_valid = slot_live[:, None] & (positions < slot_length[:, None])
    slot_rows = slot_live[:, None] & (request_order[None, :] == slot_owner[:, None])
    rows_half = slot_rows.astype(jnp.bfloat16)
    rows_wide = slot_rows.astype(jnp.float32)
    slot_query = jnp.einsum(
        "pb,sbc->psc",
        rows_half,
        queries.reshape(steps, requests, local_width),
        preferred_element_type=jnp.float32,
    ).astype(jnp.bfloat16)
    slot_query = slot_query.reshape(slot_count, steps, local_heads, HEAD_DIM)
    cache_keys = self_cache[:, 0].reshape(slot_count, page_width, local_heads, HEAD_DIM)
    cache_values = self_cache[:, 1].reshape(slot_count, page_width, local_heads, HEAD_DIM)
    cache_scores = jnp.einsum(
        "pshd,pkhd->pshk", slot_query, cache_keys, preferred_element_type=jnp.float32
    )
    valid_grid = slot_valid[:, None, None, :]
    slot_max = jnp.max(jnp.where(valid_grid, cache_scores, NEG_FILL), axis=3)
    row_max = jnp.max(
        jnp.where(slot_rows[:, None, :, None], slot_max[:, :, None, :], NEG_FILL), axis=0
    )
    causal = jnp.arange(steps)[None, :] <= jnp.arange(steps)[:, None]
    new_scores = jnp.einsum(
        "tbhd,ubhd->bhtu", query_grid, key_grid, preferred_element_type=jnp.float32
    )
    new_scores = jnp.where(causal, new_scores, NEG_FILL)
    new_max = jnp.transpose(jnp.max(new_scores, axis=3), (2, 0, 1))
    local_top = jnp.maximum(row_max, new_max)
    slot_top = jnp.einsum("pb,sbh->psh", rows_wide, local_top, precision=lax.Precision.HIGHEST)
    cache_weights = jnp.exp(jnp.where(valid_grid, cache_scores - slot_top[..., None], NEG_FILL))
    cache_denom = jnp.sum(cache_weights, axis=3)
    cache_numer = jnp.einsum(
        "pshk,pkhd->pshd",
        cache_weights.astype(jnp.bfloat16),
        cache_values,
        preferred_element_type=jnp.float32,
    )
    row_denom = jnp.einsum("pb,psh->sbh", rows_wide, cache_denom, precision=lax.Precision.HIGHEST)
    row_numer = jnp.einsum("pb,pshd->sbhd", rows_wide, cache_numer, precision=lax.Precision.HIGHEST)
    top, total_denom, total_numer = combine_seq(local_top, row_denom, row_numer, seq_size)
    top_new = jnp.transpose(top, (1, 2, 0))[..., None]
    new_weights = jnp.where(causal, jnp.exp(new_scores - top_new), 0.0)
    new_denom = jnp.transpose(jnp.sum(new_weights, axis=3), (2, 0, 1))
    new_numer = jnp.einsum(
        "bhtu,ubhd->tbhd",
        new_weights.astype(jnp.bfloat16),
        value_grid,
        preferred_element_type=jnp.float32,
    )
    self_attn = ((total_numer + new_numer) / (total_denom + new_denom)[..., None]).astype(
        jnp.bfloat16
    )
    partial_value = jnp.dot(
        self_attn.reshape(steps * requests, local_width),
        self_output,
        preferred_element_type=jnp.float32,
    )
    first_full, first_share = reduce_norm(flat, partial_value, norm_self)
    cross_queries = (
        jnp.dot(first_full, cross_query, preferred_element_type=jnp.float32) * scaling
    ).astype(jnp.bfloat16)
    cross_grid = cross_queries.reshape(steps, requests, local_heads, HEAD_DIM)
    order_rows = (request_order[:, None] == request_ids[None, :]).astype(jnp.bfloat16)
    request_query = jnp.einsum(
        "br,sbhd->srhd", order_rows, cross_grid, preferred_element_type=jnp.float32
    ).astype(jnp.bfloat16)
    enc_local = cross_cache.shape[2]
    enc_keys = cross_cache[:, 0].reshape(requests, enc_local, local_heads, HEAD_DIM)
    enc_values = cross_cache[:, 1].reshape(requests, enc_local, local_heads, HEAD_DIM)
    enc_positions = seq_index * enc_local + jnp.arange(enc_local, dtype=jnp.int32)
    enc_valid = (enc_positions[None, :] < encoder_lengths[:, None])[None, :, None, :]
    enc_scores = jnp.einsum(
        "srhd,rehd->srhe", request_query, enc_keys, preferred_element_type=jnp.float32
    )
    enc_local_top = jnp.max(jnp.where(enc_valid, enc_scores, NEG_FILL), axis=3)
    enc_weights = jnp.exp(jnp.where(enc_valid, enc_scores - enc_local_top[..., None], NEG_FILL))
    enc_numer_local = jnp.einsum(
        "srhe,rehd->srhd",
        enc_weights.astype(jnp.bfloat16),
        enc_values,
        preferred_element_type=jnp.float32,
    )
    enc_top, enc_denom, enc_numer = combine_seq(
        enc_local_top, jnp.sum(enc_weights, axis=3), enc_numer_local, seq_size
    )
    enc_attn = (enc_numer / enc_denom[..., None]).astype(jnp.bfloat16)
    cross_attn = jnp.einsum(
        "br,srhd->sbhd", order_rows, enc_attn, preferred_element_type=jnp.float32
    ).astype(jnp.bfloat16)
    partial_value = jnp.dot(
        cross_attn.reshape(steps * requests, local_width),
        cross_output,
        preferred_element_type=jnp.float32,
    )
    second_full, second_share = reduce_norm(first_full, partial_value, norm_cross)
    ffn_hidden = jax.nn.gelu(
        jnp.dot(second_full, feed_up, preferred_element_type=jnp.float32), approximate=False
    ).astype(jnp.bfloat16)
    ignored, out_share = reduce_norm(
        second_full, jnp.dot(ffn_hidden, feed_down, preferred_element_type=jnp.float32), norm_feed
    )
    return out_share.reshape(steps, requests, out_share.shape[1])


def solution(mesh):
    in_specs = (
        P(None, None, "tensor"),
        P(None, "tensor"),
        P(None, "tensor"),
        P(None, "tensor"),
        P("tensor", None),
        P(None, "tensor"),
        P("tensor", None),
        P(None, "tensor"),
        P("tensor", None),
        P(),
        P(),
        P(),
        P("seq", None, None, "tensor"),
        P(None, None, "seq", "tensor"),
        P(),
        P(),
        P(),
        P(),
    )
    out_specs = P(None, None, "tensor")
    return jax.shard_map(
        on_device, mesh=mesh, in_specs=in_specs, out_specs=out_specs, check_vma=False
    )
```

```python
import jax
import jax.numpy as jnp
from jax import lax
from jax.sharding import PartitionSpec as P

HEAD_DIM = 64


EPSILON = 1e-05
NEG_FILL = -1e30


def layer_norm(summed, gain):
    center = jnp.mean(summed, axis=-1, keepdims=True)
    spread = jnp.mean(summed * summed, axis=-1, keepdims=True) - center * center
    return (summed - center) * lax.rsqrt(spread + EPSILON) * gain


def combine_seq(top, denom, numer, size):
    index = lax.axis_index("seq")
    distance = 1
    while distance < size:
        pairs = [(i, i ^ distance) for i in range(size)]
        other_top, other_denom, other_numer = lax.ppermute((top, denom, numer), "seq", pairs)
        low = (index & distance) == 0
        top_a = jnp.where(low, top, other_top)
        top_b = jnp.where(low, other_top, top)
        denom_a = jnp.where(low, denom, other_denom)
        denom_b = jnp.where(low, other_denom, denom)
        numer_a = jnp.where(low, numer, other_numer)
        numer_b = jnp.where(low, other_numer, numer)
        merged = jnp.maximum(top_a, top_b)
        scale_a = jnp.exp(top_a - merged)
        scale_b = jnp.exp(top_b - merged)
        denom = denom_a * scale_a + denom_b * scale_b
        numer = numer_a * scale_a[..., None] + numer_b * scale_b[..., None]
        top = merged
        distance *= 2
    return top, denom, numer


def full_norm(residual, value, gain):
    return layer_norm(residual.astype(jnp.float32) + value, gain).astype(jnp.bfloat16)


def gather_columns(block):
    return lax.all_gather(block, "tensor", axis=1, tiled=True)


def on_device(
    new_states,
    self_query,
    self_key,
    self_value,
    self_output,
    cross_query,
    cross_output,
    feed_up,
    feed_down,
    norm_self,
    norm_cross,
    norm_feed,
    self_cache,
    cross_cache,
    cache_lengths,
    page_table,
    request_order,
    encoder_lengths,
):
    states = lax.all_gather(new_states, "tensor", axis=2, tiled=True)
    self_output = lax.all_gather(self_output, "tensor", axis=0, tiled=True)
    cross_output = lax.all_gather(cross_output, "tensor", axis=0, tiled=True)
    steps, requests, width = states.shape
    flat = states.reshape(steps * requests, width)
    local_width = self_query.shape[1]
    local_heads = local_width // HEAD_DIM
    scaling = HEAD_DIM ** (-0.5)
    queries = (jnp.dot(flat, self_query, preferred_element_type=jnp.float32) * scaling).astype(
        jnp.bfloat16
    )
    new_keys = jnp.dot(flat, self_key, preferred_element_type=jnp.float32).astype(jnp.bfloat16)
    new_values = jnp.dot(flat, self_value, preferred_element_type=jnp.float32).astype(jnp.bfloat16)
    query_grid = queries.reshape(steps, requests, local_heads, HEAD_DIM)
    key_grid = new_keys.reshape(steps, requests, local_heads, HEAD_DIM)
    value_grid = new_values.reshape(steps, requests, local_heads, HEAD_DIM)
    slot_count = self_cache.shape[0]
    page_width = self_cache.shape[2]
    max_pages = page_table.shape[1]
    seq_index = lax.axis_index("seq")
    seq_size = lax.axis_size("seq")
    flat_table = page_table.reshape(-1)
    entry_ids = jnp.arange(requests * max_pages, dtype=jnp.int32)
    entry_request = entry_ids // max_pages
    entry_page = entry_ids % max_pages
    slot_ids = seq_index * slot_count + jnp.arange(slot_count, dtype=jnp.int32)
    matches = flat_table[None, :] == slot_ids[:, None]
    slot_live = jnp.any(matches, axis=1)
    slot_owner = jnp.sum(jnp.where(matches, entry_request[None, :], 0), axis=1)
    slot_page = jnp.sum(jnp.where(matches, entry_page[None, :], 0), axis=1)
    request_ids = jnp.arange(requests, dtype=jnp.int32)
    slot_length = jnp.sum(
        jnp.where(slot_owner[:, None] == request_ids[None, :], cache_lengths[None, :], 0), axis=1
    )
    positions = slot_page[:, None] * page_width + jnp.arange(page_width, dtype=jnp.int32)[None, :]
    slot_valid = slot_live[:, None] & (positions < slot_length[:, None])
    slot_rows = slot_live[:, None] & (request_order[None, :] == slot_owner[:, None])
    rows_half = slot_rows.astype(jnp.bfloat16)
    rows_wide = slot_rows.astype(jnp.float32)
    slot_query = jnp.einsum(
        "pb,sbc->psc",
        rows_half,
        queries.reshape(steps, requests, local_width),
        preferred_element_type=jnp.float32,
    ).astype(jnp.bfloat16)
    slot_query = slot_query.reshape(slot_count, steps, local_heads, HEAD_DIM)
    cache_keys = self_cache[:, 0].reshape(slot_count, page_width, local_heads, HEAD_DIM)
    cache_values = self_cache[:, 1].reshape(slot_count, page_width, local_heads, HEAD_DIM)
    cache_scores = jnp.einsum(
        "pshd,pkhd->pshk", slot_query, cache_keys, preferred_element_type=jnp.float32
    )
    valid_grid = slot_valid[:, None, None, :]
    slot_max = jnp.max(jnp.where(valid_grid, cache_scores, NEG_FILL), axis=3)
    row_max = jnp.max(
        jnp.where(slot_rows[:, None, :, None], slot_max[:, :, None, :], NEG_FILL), axis=0
    )
    causal = jnp.arange(steps)[None, :] <= jnp.arange(steps)[:, None]
    new_scores = jnp.einsum(
        "tbhd,ubhd->bhtu", query_grid, key_grid, preferred_element_type=jnp.float32
    )
    new_scores = jnp.where(causal, new_scores, NEG_FILL)
    new_max = jnp.transpose(jnp.max(new_scores, axis=3), (2, 0, 1))
    local_top = jnp.maximum(row_max, new_max)
    slot_top = jnp.einsum("pb,sbh->psh", rows_wide, local_top, precision=lax.Precision.HIGHEST)
    cache_weights = jnp.exp(jnp.where(valid_grid, cache_scores - slot_top[..., None], NEG_FILL))
    cache_denom = jnp.sum(cache_weights, axis=3)
    cache_numer = jnp.einsum(
        "pshk,pkhd->pshd",
        cache_weights.astype(jnp.bfloat16),
        cache_values,
        preferred_element_type=jnp.float32,
    )
    row_denom = jnp.einsum("pb,psh->sbh", rows_wide, cache_denom, precision=lax.Precision.HIGHEST)
    row_numer = jnp.einsum("pb,pshd->sbhd", rows_wide, cache_numer, precision=lax.Precision.HIGHEST)
    top, total_denom, total_numer = combine_seq(local_top, row_denom, row_numer, seq_size)
    top_new = jnp.transpose(top, (1, 2, 0))[..., None]
    new_weights = jnp.where(causal, jnp.exp(new_scores - top_new), 0.0)
    new_denom = jnp.transpose(jnp.sum(new_weights, axis=3), (2, 0, 1))
    new_numer = jnp.einsum(
        "bhtu,ubhd->tbhd",
        new_weights.astype(jnp.bfloat16),
        value_grid,
        preferred_element_type=jnp.float32,
    )
    self_attn = ((total_numer + new_numer) / (total_denom + new_denom)[..., None]).astype(
        jnp.bfloat16
    )
    attn_value = jnp.dot(
        gather_columns(self_attn.reshape(steps * requests, local_width)),
        self_output,
        preferred_element_type=jnp.float32,
    )
    first_full = full_norm(flat, attn_value, norm_self)
    cross_queries = (
        jnp.dot(first_full, cross_query, preferred_element_type=jnp.float32) * scaling
    ).astype(jnp.bfloat16)
    cross_grid = cross_queries.reshape(steps, requests, local_heads, HEAD_DIM)
    order_rows = (request_order[:, None] == request_ids[None, :]).astype(jnp.bfloat16)
    request_query = jnp.einsum(
        "br,sbhd->srhd", order_rows, cross_grid, preferred_element_type=jnp.float32
    ).astype(jnp.bfloat16)
    enc_local = cross_cache.shape[2]
    enc_keys = cross_cache[:, 0].reshape(requests, enc_local, local_heads, HEAD_DIM)
    enc_values = cross_cache[:, 1].reshape(requests, enc_local, local_heads, HEAD_DIM)
    enc_positions = seq_index * enc_local + jnp.arange(enc_local, dtype=jnp.int32)
    enc_valid = (enc_positions[None, :] < encoder_lengths[:, None])[None, :, None, :]
    enc_scores = jnp.einsum(
        "srhd,rehd->srhe", request_query, enc_keys, preferred_element_type=jnp.float32
    )
    enc_local_top = jnp.max(jnp.where(enc_valid, enc_scores, NEG_FILL), axis=3)
    enc_weights = jnp.exp(jnp.where(enc_valid, enc_scores - enc_local_top[..., None], NEG_FILL))
    enc_numer_local = jnp.einsum(
        "srhe,rehd->srhd",
        enc_weights.astype(jnp.bfloat16),
        enc_values,
        preferred_element_type=jnp.float32,
    )
    enc_top, enc_denom, enc_numer = combine_seq(
        enc_local_top, jnp.sum(enc_weights, axis=3), enc_numer_local, seq_size
    )
    enc_attn = (enc_numer / enc_denom[..., None]).astype(jnp.bfloat16)
    cross_attn = jnp.einsum(
        "br,srhd->sbhd", order_rows, enc_attn, preferred_element_type=jnp.float32
    ).astype(jnp.bfloat16)
    attn_value = jnp.dot(
        gather_columns(cross_attn.reshape(steps * requests, local_width)),
        cross_output,
        preferred_element_type=jnp.float32,
    )
    second_full = full_norm(first_full, attn_value, norm_cross)
    ffn_hidden = jax.nn.gelu(
        jnp.dot(second_full, feed_up, preferred_element_type=jnp.float32), approximate=False
    ).astype(jnp.bfloat16)
    ffn_value = lax.psum(
        jnp.dot(ffn_hidden, feed_down, preferred_element_type=jnp.float32), "tensor"
    )
    out_full = full_norm(second_full, ffn_value, norm_feed)
    out_share = lax.dynamic_slice_in_dim(
        out_full, lax.axis_index("tensor") * local_width, local_width, 1
    )
    return out_share.reshape(steps, requests, local_width)


def solution(mesh):
    in_specs = (
        P(None, None, "tensor"),
        P(None, "tensor"),
        P(None, "tensor"),
        P(None, "tensor"),
        P("tensor", None),
        P(None, "tensor"),
        P("tensor", None),
        P(None, "tensor"),
        P("tensor", None),
        P(),
        P(),
        P(),
        P("seq", None, None, "tensor"),
        P(None, None, "seq", "tensor"),
        P(),
        P(),
        P(),
        P(),
    )
    out_specs = P(None, None, "tensor")
    return jax.shard_map(
        on_device, mesh=mesh, in_specs=in_specs, out_specs=out_specs, check_vma=False
    )
```

```python
import jax
import jax.numpy as jnp
from jax import lax
from jax.sharding import PartitionSpec as P

HEAD_DIM = 64


EPSILON = 1e-05
NEG_FILL = -1e30


def layer_norm(summed, gain):
    center = jnp.mean(summed, axis=-1, keepdims=True)
    spread = jnp.mean(summed * summed, axis=-1, keepdims=True) - center * center
    return (summed - center) * lax.rsqrt(spread + EPSILON) * gain


def combine_seq(top, denom, numer, size):
    index = lax.axis_index("seq")
    distance = 1
    while distance < size:
        pairs = [(i, i ^ distance) for i in range(size)]
        other_top, other_denom, other_numer = lax.ppermute((top, denom, numer), "seq", pairs)
        low = (index & distance) == 0
        top_a = jnp.where(low, top, other_top)
        top_b = jnp.where(low, other_top, top)
        denom_a = jnp.where(low, denom, other_denom)
        denom_b = jnp.where(low, other_denom, denom)
        numer_a = jnp.where(low, numer, other_numer)
        numer_b = jnp.where(low, other_numer, numer)
        merged = jnp.maximum(top_a, top_b)
        scale_a = jnp.exp(top_a - merged)
        scale_b = jnp.exp(top_b - merged)
        denom = denom_a * scale_a + denom_b * scale_b
        numer = numer_a * scale_a[..., None] + numer_b * scale_b[..., None]
        top = merged
        distance *= 2
    return top, denom, numer


def full_norm(residual, value, gain):
    return layer_norm(residual.astype(jnp.float32) + value, gain).astype(jnp.bfloat16)


def from_tensor_offset(block, offset, size):
    return lax.ppermute(block, "tensor", [(i, (i - offset) % size) for i in range(size)])


def in_device_order(pieces):
    stacked = jnp.stack(pieces)
    return jnp.roll(stacked, lax.axis_index("tensor"), axis=0)


def gather_tensor(block, axis):
    size = lax.axis_size("tensor")
    pieces = [block] + [from_tensor_offset(block, k, size) for k in range(1, size)]
    ordered = in_device_order(pieces)
    return jnp.concatenate([ordered[j] for j in range(size)], axis=axis)


def gather_columns(block):
    return gather_tensor(block, 1)


def reduce_rows_norm(residual, partial_value, gain):
    size = lax.axis_size("tensor")
    me = lax.axis_index("tensor")
    rows = partial_value.shape[0] // size
    columns = partial_value.shape[1] // size

    def rows_of(value, owner):
        return lax.dynamic_slice_in_dim(value, owner * rows, rows, 0)

    total = rows_of(partial_value, me)
    for k in range(1, size):
        total = total + from_tensor_offset(rows_of(partial_value, (me - k) % size), k, size)
    normed = full_norm(rows_of(residual, me), total, gain)
    pieces = [lax.dynamic_slice_in_dim(normed, me * columns, columns, 1)]
    for k in range(1, size):
        target = (me - k) % size
        pieces.append(
            from_tensor_offset(
                lax.dynamic_slice_in_dim(normed, target * columns, columns, 1), k, size
            )
        )
    ordered = in_device_order(pieces)
    return jnp.concatenate([ordered[j] for j in range(size)], axis=0)


def on_device(
    new_states,
    self_query,
    self_key,
    self_value,
    self_output,
    cross_query,
    cross_output,
    feed_up,
    feed_down,
    norm_self,
    norm_cross,
    norm_feed,
    self_cache,
    cross_cache,
    cache_lengths,
    page_table,
    request_order,
    encoder_lengths,
):
    states = gather_tensor(new_states, 2)
    self_output = gather_tensor(self_output, 0)
    cross_output = gather_tensor(cross_output, 0)
    steps, requests, width = states.shape
    flat = states.reshape(steps * requests, width)
    local_width = self_query.shape[1]
    local_heads = local_width // HEAD_DIM
    scaling = HEAD_DIM ** (-0.5)
    queries = (jnp.dot(flat, self_query, preferred_element_type=jnp.float32) * scaling).astype(
        jnp.bfloat16
    )
    new_keys = jnp.dot(flat, self_key, preferred_element_type=jnp.float32).astype(jnp.bfloat16)
    new_values = jnp.dot(flat, self_value, preferred_element_type=jnp.float32).astype(jnp.bfloat16)
    query_grid = queries.reshape(steps, requests, local_heads, HEAD_DIM)
    key_grid = new_keys.reshape(steps, requests, local_heads, HEAD_DIM)
    value_grid = new_values.reshape(steps, requests, local_heads, HEAD_DIM)
    slot_count = self_cache.shape[0]
    page_width = self_cache.shape[2]
    max_pages = page_table.shape[1]
    seq_index = lax.axis_index("seq")
    seq_size = lax.axis_size("seq")
    flat_table = page_table.reshape(-1)
    entry_ids = jnp.arange(requests * max_pages, dtype=jnp.int32)
    entry_request = entry_ids // max_pages
    entry_page = entry_ids % max_pages
    slot_ids = seq_index * slot_count + jnp.arange(slot_count, dtype=jnp.int32)
    matches = flat_table[None, :] == slot_ids[:, None]
    slot_live = jnp.any(matches, axis=1)
    slot_owner = jnp.sum(jnp.where(matches, entry_request[None, :], 0), axis=1)
    slot_page = jnp.sum(jnp.where(matches, entry_page[None, :], 0), axis=1)
    request_ids = jnp.arange(requests, dtype=jnp.int32)
    slot_length = jnp.sum(
        jnp.where(slot_owner[:, None] == request_ids[None, :], cache_lengths[None, :], 0), axis=1
    )
    positions = slot_page[:, None] * page_width + jnp.arange(page_width, dtype=jnp.int32)[None, :]
    slot_valid = slot_live[:, None] & (positions < slot_length[:, None])
    slot_rows = slot_live[:, None] & (request_order[None, :] == slot_owner[:, None])
    rows_half = slot_rows.astype(jnp.bfloat16)
    rows_wide = slot_rows.astype(jnp.float32)
    slot_query = jnp.einsum(
        "pb,sbc->psc",
        rows_half,
        queries.reshape(steps, requests, local_width),
        preferred_element_type=jnp.float32,
    ).astype(jnp.bfloat16)
    slot_query = slot_query.reshape(slot_count, steps, local_heads, HEAD_DIM)
    cache_keys = self_cache[:, 0].reshape(slot_count, page_width, local_heads, HEAD_DIM)
    cache_values = self_cache[:, 1].reshape(slot_count, page_width, local_heads, HEAD_DIM)
    cache_scores = jnp.einsum(
        "pshd,pkhd->pshk", slot_query, cache_keys, preferred_element_type=jnp.float32
    )
    valid_grid = slot_valid[:, None, None, :]
    slot_max = jnp.max(jnp.where(valid_grid, cache_scores, NEG_FILL), axis=3)
    row_max = jnp.max(
        jnp.where(slot_rows[:, None, :, None], slot_max[:, :, None, :], NEG_FILL), axis=0
    )
    causal = jnp.arange(steps)[None, :] <= jnp.arange(steps)[:, None]
    new_scores = jnp.einsum(
        "tbhd,ubhd->bhtu", query_grid, key_grid, preferred_element_type=jnp.float32
    )
    new_scores = jnp.where(causal, new_scores, NEG_FILL)
    new_max = jnp.transpose(jnp.max(new_scores, axis=3), (2, 0, 1))
    local_top = jnp.maximum(row_max, new_max)
    slot_top = jnp.einsum("pb,sbh->psh", rows_wide, local_top, precision=lax.Precision.HIGHEST)
    cache_weights = jnp.exp(jnp.where(valid_grid, cache_scores - slot_top[..., None], NEG_FILL))
    cache_denom = jnp.sum(cache_weights, axis=3)
    cache_numer = jnp.einsum(
        "pshk,pkhd->pshd",
        cache_weights.astype(jnp.bfloat16),
        cache_values,
        preferred_element_type=jnp.float32,
    )
    row_denom = jnp.einsum("pb,psh->sbh", rows_wide, cache_denom, precision=lax.Precision.HIGHEST)
    row_numer = jnp.einsum("pb,pshd->sbhd", rows_wide, cache_numer, precision=lax.Precision.HIGHEST)
    top, total_denom, total_numer = combine_seq(local_top, row_denom, row_numer, seq_size)
    top_new = jnp.transpose(top, (1, 2, 0))[..., None]
    new_weights = jnp.where(causal, jnp.exp(new_scores - top_new), 0.0)
    new_denom = jnp.transpose(jnp.sum(new_weights, axis=3), (2, 0, 1))
    new_numer = jnp.einsum(
        "bhtu,ubhd->tbhd",
        new_weights.astype(jnp.bfloat16),
        value_grid,
        preferred_element_type=jnp.float32,
    )
    self_attn = ((total_numer + new_numer) / (total_denom + new_denom)[..., None]).astype(
        jnp.bfloat16
    )
    attn_value = jnp.dot(
        gather_columns(self_attn.reshape(steps * requests, local_width)),
        self_output,
        preferred_element_type=jnp.float32,
    )
    first_full = full_norm(flat, attn_value, norm_self)
    cross_queries = (
        jnp.dot(first_full, cross_query, preferred_element_type=jnp.float32) * scaling
    ).astype(jnp.bfloat16)
    cross_grid = cross_queries.reshape(steps, requests, local_heads, HEAD_DIM)
    order_rows = (request_order[:, None] == request_ids[None, :]).astype(jnp.bfloat16)
    request_query = jnp.einsum(
        "br,sbhd->srhd", order_rows, cross_grid, preferred_element_type=jnp.float32
    ).astype(jnp.bfloat16)
    enc_local = cross_cache.shape[2]
    enc_keys = cross_cache[:, 0].reshape(requests, enc_local, local_heads, HEAD_DIM)
    enc_values = cross_cache[:, 1].reshape(requests, enc_local, local_heads, HEAD_DIM)
    enc_positions = seq_index * enc_local + jnp.arange(enc_local, dtype=jnp.int32)
    enc_valid = (enc_positions[None, :] < encoder_lengths[:, None])[None, :, None, :]
    enc_scores = jnp.einsum(
        "srhd,rehd->srhe", request_query, enc_keys, preferred_element_type=jnp.float32
    )
    enc_local_top = jnp.max(jnp.where(enc_valid, enc_scores, NEG_FILL), axis=3)
    enc_weights = jnp.exp(jnp.where(enc_valid, enc_scores - enc_local_top[..., None], NEG_FILL))
    enc_numer_local = jnp.einsum(
        "srhe,rehd->srhd",
        enc_weights.astype(jnp.bfloat16),
        enc_values,
        preferred_element_type=jnp.float32,
    )
    enc_top, enc_denom, enc_numer = combine_seq(
        enc_local_top, jnp.sum(enc_weights, axis=3), enc_numer_local, seq_size
    )
    enc_attn = (enc_numer / enc_denom[..., None]).astype(jnp.bfloat16)
    cross_attn = jnp.einsum(
        "br,srhd->sbhd", order_rows, enc_attn, preferred_element_type=jnp.float32
    ).astype(jnp.bfloat16)
    attn_value = jnp.dot(
        gather_columns(cross_attn.reshape(steps * requests, local_width)),
        cross_output,
        preferred_element_type=jnp.float32,
    )
    second_full = full_norm(first_full, attn_value, norm_cross)
    ffn_hidden = jax.nn.gelu(
        jnp.dot(second_full, feed_up, preferred_element_type=jnp.float32), approximate=False
    ).astype(jnp.bfloat16)
    out_share = reduce_rows_norm(
        second_full, jnp.dot(ffn_hidden, feed_down, preferred_element_type=jnp.float32), norm_feed
    )
    return out_share.reshape(steps, requests, local_width)


def solution(mesh):
    in_specs = (
        P(None, None, "tensor"),
        P(None, "tensor"),
        P(None, "tensor"),
        P(None, "tensor"),
        P("tensor", None),
        P(None, "tensor"),
        P("tensor", None),
        P(None, "tensor"),
        P("tensor", None),
        P(),
        P(),
        P(),
        P("seq", None, None, "tensor"),
        P(None, None, "seq", "tensor"),
        P(),
        P(),
        P(),
        P(),
    )
    out_specs = P(None, None, "tensor")
    return jax.shard_map(
        on_device, mesh=mesh, in_specs=in_specs, out_specs=out_specs, check_vma=False
    )
```

```python
import jax
import jax.numpy as jnp
from jax import lax
from jax.sharding import PartitionSpec as P

HEAD_DIM = 64


EPSILON = 1e-05
NEG_FILL = -1e30


def layer_norm(summed, gain):
    center = jnp.mean(summed, axis=-1, keepdims=True)
    spread = jnp.mean(summed * summed, axis=-1, keepdims=True) - center * center
    return (summed - center) * lax.rsqrt(spread + EPSILON) * gain


def merge_partials(low, high):
    top_a, denom_a, numer_a = low
    top_b, denom_b, numer_b = high
    top = jnp.maximum(top_a, top_b)
    scale_a = jnp.exp(top_a - top)
    scale_b = jnp.exp(top_b - top)
    denom = denom_a * scale_a + denom_b * scale_b
    numer = numer_a * scale_a[..., None] + numer_b * scale_b[..., None]
    return top, denom, numer


def scatter_seq(parts, size):
    index = lax.axis_index("seq")
    distance = 1
    while distance < size:
        half = parts[0].shape[0] // 2
        upper = (index & distance) != 0
        keep = jnp.where(upper, half, 0)
        give = half - keep
        mine = tuple(lax.dynamic_slice_in_dim(x, keep, half, 0) for x in parts)
        sent = tuple(lax.dynamic_slice_in_dim(x, give, half, 0) for x in parts)
        theirs = lax.ppermute(sent, "seq", [(i, i ^ distance) for i in range(size)])
        low = tuple(jnp.where(upper, t, m) for m, t in zip(mine, theirs))
        high = tuple(jnp.where(upper, m, t) for m, t in zip(mine, theirs))
        parts = merge_partials(low, high)
        distance *= 2
    return parts


def gather_seq(block, size):
    index = lax.axis_index("seq")
    distance = size // 2
    while distance >= 1:
        theirs = lax.ppermute(block, "seq", [(i, i ^ distance) for i in range(size)])
        upper = (index & distance) != 0
        block = jnp.where(
            upper, jnp.concatenate([theirs, block]), jnp.concatenate([block, theirs])
        )
        distance //= 2
    return block


def softmax_rows(top, denom, numer, size):
    rows = top.shape[0] * top.shape[1]
    heads = top.shape[2]
    parts = (top.reshape(rows, heads), denom.reshape(rows, heads), numer.reshape(rows, heads, -1))
    top, denom, numer = scatter_seq(parts, size)
    block = (numer / denom[..., None]).astype(jnp.bfloat16)
    return gather_seq(block.reshape(block.shape[0], -1), size)


def full_norm(residual, value, gain):
    return layer_norm(residual.astype(jnp.float32) + value, gain).astype(jnp.bfloat16)


def from_tensor_offset(block, offset, size):
    return lax.ppermute(block, "tensor", [(i, (i - offset) % size) for i in range(size)])


def in_device_order(pieces):
    stacked = jnp.stack(pieces)
    return jnp.roll(stacked, lax.axis_index("tensor"), axis=0)


def gather_tensor(block, axis):
    size = lax.axis_size("tensor")
    pieces = [block] + [from_tensor_offset(block, k, size) for k in range(1, size)]
    ordered = in_device_order(pieces)
    return jnp.concatenate([ordered[j] for j in range(size)], axis=axis)


def gather_columns(block):
    return gather_tensor(block, 1)


def reduce_rows_norm(residual, partial_value, gain):
    size = lax.axis_size("tensor")
    me = lax.axis_index("tensor")
    rows = partial_value.shape[0] // size
    columns = partial_value.shape[1] // size

    def rows_of(value, owner):
        return lax.dynamic_slice_in_dim(value, owner * rows, rows, 0)

    total = rows_of(partial_value, me)
    for k in range(1, size):
        total = total + from_tensor_offset(rows_of(partial_value, (me - k) % size), k, size)
    normed = full_norm(rows_of(residual, me), total, gain)
    pieces = [lax.dynamic_slice_in_dim(normed, me * columns, columns, 1)]
    for k in range(1, size):
        target = (me - k) % size
        pieces.append(
            from_tensor_offset(
                lax.dynamic_slice_in_dim(normed, target * columns, columns, 1), k, size
            )
        )
    ordered = in_device_order(pieces)
    return jnp.concatenate([ordered[j] for j in range(size)], axis=0)


def on_device(
    new_states,
    self_query,
    self_key,
    self_value,
    self_output,
    cross_query,
    cross_output,
    feed_up,
    feed_down,
    norm_self,
    norm_cross,
    norm_feed,
    self_cache,
    cross_cache,
    cache_lengths,
    page_table,
    request_order,
    encoder_lengths,
):
    states = gather_tensor(new_states, 2)
    self_output = gather_tensor(self_output, 0)
    cross_output = gather_tensor(cross_output, 0)
    steps, requests, width = states.shape
    flat = states.reshape(steps * requests, width)
    local_width = self_query.shape[1]
    local_heads = local_width // HEAD_DIM
    scaling = HEAD_DIM ** (-0.5)
    queries = (jnp.dot(flat, self_query, preferred_element_type=jnp.float32) * scaling).astype(
        jnp.bfloat16
    )
    new_keys = jnp.dot(flat, self_key, preferred_element_type=jnp.float32).astype(jnp.bfloat16)
    new_values = jnp.dot(flat, self_value, preferred_element_type=jnp.float32).astype(jnp.bfloat16)
    query_grid = queries.reshape(steps, requests, local_heads, HEAD_DIM)
    key_grid = new_keys.reshape(steps, requests, local_heads, HEAD_DIM)
    value_grid = new_values.reshape(steps, requests, local_heads, HEAD_DIM)
    slot_count = self_cache.shape[0]
    page_width = self_cache.shape[2]
    max_pages = page_table.shape[1]
    seq_index = lax.axis_index("seq")
    seq_size = lax.axis_size("seq")
    flat_table = page_table.reshape(-1)
    entry_ids = jnp.arange(requests * max_pages, dtype=jnp.int32)
    entry_request = entry_ids // max_pages
    entry_page = entry_ids % max_pages
    slot_ids = seq_index * slot_count + jnp.arange(slot_count, dtype=jnp.int32)
    matches = flat_table[None, :] == slot_ids[:, None]
    slot_live = jnp.any(matches, axis=1)
    slot_owner = jnp.sum(jnp.where(matches, entry_request[None, :], 0), axis=1)
    slot_page = jnp.sum(jnp.where(matches, entry_page[None, :], 0), axis=1)
    request_ids = jnp.arange(requests, dtype=jnp.int32)
    slot_length = jnp.sum(
        jnp.where(slot_owner[:, None] == request_ids[None, :], cache_lengths[None, :], 0), axis=1
    )
    positions = slot_page[:, None] * page_width + jnp.arange(page_width, dtype=jnp.int32)[None, :]
    slot_valid = slot_live[:, None] & (positions < slot_length[:, None])
    slot_rows = slot_live[:, None] & (request_order[None, :] == slot_owner[:, None])
    rows_half = slot_rows.astype(jnp.bfloat16)
    rows_wide = slot_rows.astype(jnp.float32)
    slot_query = jnp.einsum(
        "pb,sbc->psc",
        rows_half,
        queries.reshape(steps, requests, local_width),
        preferred_element_type=jnp.float32,
    ).astype(jnp.bfloat16)
    slot_query = slot_query.reshape(slot_count, steps, local_heads, HEAD_DIM)
    cache_keys = self_cache[:, 0].reshape(slot_count, page_width, local_heads, HEAD_DIM)
    cache_values = self_cache[:, 1].reshape(slot_count, page_width, local_heads, HEAD_DIM)
    cache_scores = jnp.einsum(
        "pshd,pkhd->pshk", slot_query, cache_keys, preferred_element_type=jnp.float32
    )
    valid_grid = slot_valid[:, None, None, :]
    slot_max = jnp.max(jnp.where(valid_grid, cache_scores, NEG_FILL), axis=3)
    row_max = jnp.max(
        jnp.where(slot_rows[:, None, :, None], slot_max[:, :, None, :], NEG_FILL), axis=0
    )
    causal = jnp.arange(steps)[None, :] <= jnp.arange(steps)[:, None]
    new_scores = jnp.einsum(
        "tbhd,ubhd->bhtu", query_grid, key_grid, preferred_element_type=jnp.float32
    )
    new_scores = jnp.where(causal, new_scores, NEG_FILL)
    new_max = jnp.transpose(jnp.max(new_scores, axis=3), (2, 0, 1))
    first = seq_index == 0
    local_top = jnp.where(first, jnp.maximum(row_max, new_max), row_max)
    slot_top = jnp.einsum("pb,sbh->psh", rows_wide, local_top, precision=lax.Precision.HIGHEST)
    cache_weights = jnp.exp(jnp.where(valid_grid, cache_scores - slot_top[..., None], NEG_FILL))
    cache_denom = jnp.sum(cache_weights, axis=3)
    cache_numer = jnp.einsum(
        "pshk,pkhd->pshd",
        cache_weights.astype(jnp.bfloat16),
        cache_values,
        preferred_element_type=jnp.float32,
    )
    row_denom = jnp.einsum("pb,psh->sbh", rows_wide, cache_denom, precision=lax.Precision.HIGHEST)
    row_numer = jnp.einsum("pb,pshd->sbhd", rows_wide, cache_numer, precision=lax.Precision.HIGHEST)
    new_top = jnp.maximum(local_top, new_max)
    top_new = jnp.transpose(new_top, (1, 2, 0))[..., None]
    new_weights = jnp.where(causal, jnp.exp(new_scores - top_new), 0.0)
    new_denom = jnp.transpose(jnp.sum(new_weights, axis=3), (2, 0, 1))
    new_numer = jnp.einsum(
        "bhtu,ubhd->tbhd",
        new_weights.astype(jnp.bfloat16),
        value_grid,
        preferred_element_type=jnp.float32,
    )
    part_denom = row_denom + jnp.where(first, new_denom, 0.0)
    part_numer = row_numer + jnp.where(first, new_numer, 0.0)
    self_attn = softmax_rows(local_top, part_denom, part_numer, seq_size)
    attn_value = jnp.dot(
        gather_columns(self_attn),
        self_output,
        preferred_element_type=jnp.float32,
    )
    first_full = full_norm(flat, attn_value, norm_self)
    cross_queries = (
        jnp.dot(first_full, cross_query, preferred_element_type=jnp.float32) * scaling
    ).astype(jnp.bfloat16)
    cross_grid = cross_queries.reshape(steps, requests, local_heads, HEAD_DIM)
    order_rows = (request_order[:, None] == request_ids[None, :]).astype(jnp.bfloat16)
    request_query = jnp.einsum(
        "br,sbhd->srhd", order_rows, cross_grid, preferred_element_type=jnp.float32
    ).astype(jnp.bfloat16)
    enc_local = cross_cache.shape[2]
    enc_keys = cross_cache[:, 0].reshape(requests, enc_local, local_heads, HEAD_DIM)
    enc_values = cross_cache[:, 1].reshape(requests, enc_local, local_heads, HEAD_DIM)
    enc_positions = seq_index * enc_local + jnp.arange(enc_local, dtype=jnp.int32)
    enc_valid = (enc_positions[None, :] < encoder_lengths[:, None])[None, :, None, :]
    enc_scores = jnp.einsum(
        "srhd,rehd->srhe", request_query, enc_keys, preferred_element_type=jnp.float32
    )
    enc_local_top = jnp.max(jnp.where(enc_valid, enc_scores, NEG_FILL), axis=3)
    enc_weights = jnp.exp(jnp.where(enc_valid, enc_scores - enc_local_top[..., None], NEG_FILL))
    enc_numer_local = jnp.einsum(
        "srhe,rehd->srhd",
        enc_weights.astype(jnp.bfloat16),
        enc_values,
        preferred_element_type=jnp.float32,
    )
    enc_attn = softmax_rows(
        enc_local_top, jnp.sum(enc_weights, axis=3), enc_numer_local, seq_size
    ).reshape(steps, requests, local_heads, HEAD_DIM)
    cross_attn = jnp.einsum(
        "br,srhd->sbhd", order_rows, enc_attn, preferred_element_type=jnp.float32
    ).astype(jnp.bfloat16)
    attn_value = jnp.dot(
        gather_columns(cross_attn.reshape(steps * requests, local_width)),
        cross_output,
        preferred_element_type=jnp.float32,
    )
    second_full = full_norm(first_full, attn_value, norm_cross)
    ffn_hidden = jax.nn.gelu(
        jnp.dot(second_full, feed_up, preferred_element_type=jnp.float32), approximate=False
    ).astype(jnp.bfloat16)
    out_share = reduce_rows_norm(
        second_full, jnp.dot(ffn_hidden, feed_down, preferred_element_type=jnp.float32), norm_feed
    )
    return out_share.reshape(steps, requests, local_width)


def solution(mesh):
    in_specs = (
        P(None, None, "tensor"),
        P(None, "tensor"),
        P(None, "tensor"),
        P(None, "tensor"),
        P("tensor", None),
        P(None, "tensor"),
        P("tensor", None),
        P(None, "tensor"),
        P("tensor", None),
        P(),
        P(),
        P(),
        P("seq", None, None, "tensor"),
        P(None, None, "seq", "tensor"),
        P(),
        P(),
        P(),
        P(),
    )
    out_specs = P(None, None, "tensor")
    return jax.shard_map(
        on_device, mesh=mesh, in_specs=in_specs, out_specs=out_specs, check_vma=False
    )
```

```python
import jax
import jax.numpy as jnp
from jax import lax
from jax.sharding import PartitionSpec as P

HEAD_DIM = 64


EPSILON = 1e-05
NEG_FILL = -1e30


def layer_norm(summed, gain):
    center = jnp.mean(summed, axis=-1, keepdims=True)
    spread = jnp.mean(summed * summed, axis=-1, keepdims=True) - center * center
    return (summed - center) * lax.rsqrt(spread + EPSILON) * gain


def merge_partials(low, high):
    top_a, denom_a, numer_a = low
    top_b, denom_b, numer_b = high
    top = jnp.maximum(top_a, top_b)
    scale_a = jnp.exp(top_a - top)
    scale_b = jnp.exp(top_b - top)
    denom = denom_a * scale_a + denom_b * scale_b
    numer = numer_a * scale_a[..., None] + numer_b * scale_b[..., None]
    return top, denom, numer


def scatter_seq(parts, size):
    index = lax.axis_index("seq")
    distance = 1
    while distance < size:
        half = parts[0].shape[0] // 2
        upper = (index & distance) != 0
        keep = jnp.where(upper, half, 0)
        give = half - keep
        mine = tuple(lax.dynamic_slice_in_dim(x, keep, half, 0) for x in parts)
        sent = tuple(lax.dynamic_slice_in_dim(x, give, half, 0) for x in parts)
        theirs = lax.ppermute(sent, "seq", [(i, i ^ distance) for i in range(size)])
        low = tuple(jnp.where(upper, t, m) for m, t in zip(mine, theirs))
        high = tuple(jnp.where(upper, m, t) for m, t in zip(mine, theirs))
        parts = merge_partials(low, high)
        distance *= 2
    return parts


def gather_seq(block, size):
    index = lax.axis_index("seq")
    distance = size // 2
    while distance >= 1:
        theirs = lax.ppermute(block, "seq", [(i, i ^ distance) for i in range(size)])
        upper = (index & distance) != 0
        block = jnp.where(
            upper, jnp.concatenate([theirs, block]), jnp.concatenate([block, theirs])
        )
        distance //= 2
    return block


def softmax_rows(top, denom, numer, size):
    rows = top.shape[0] * top.shape[1]
    heads = top.shape[2]
    parts = (top.reshape(rows, heads), denom.reshape(rows, heads), numer.reshape(rows, heads, -1))
    top, denom, numer = scatter_seq(parts, size)
    block = (numer / denom[..., None]).astype(jnp.bfloat16)
    return gather_seq(block.reshape(block.shape[0], -1), size)


def full_norm(residual, value, gain):
    return layer_norm(residual.astype(jnp.float32) + value, gain).astype(jnp.bfloat16)


def from_tensor_offset(block, offset, size):
    return lax.ppermute(block, "tensor", [(i, (i - offset) % size) for i in range(size)])


def in_device_order(pieces):
    stacked = jnp.stack(pieces)
    return jnp.roll(stacked, lax.axis_index("tensor"), axis=0)


def gather_tensor(block, axis):
    size = lax.axis_size("tensor")
    pieces = [block] + [from_tensor_offset(block, k, size) for k in range(1, size)]
    ordered = in_device_order(pieces)
    return jnp.concatenate([ordered[j] for j in range(size)], axis=axis)


def gather_columns(block):
    return gather_tensor(block, 1)


def reduce_rows_norm(residual, partial_value, gain):
    size = lax.axis_size("tensor")
    me = lax.axis_index("tensor")
    rows = partial_value.shape[0] // size
    columns = partial_value.shape[1] // size

    def rows_of(value, owner):
        return lax.dynamic_slice_in_dim(value, owner * rows, rows, 0)

    total = rows_of(partial_value, me)
    for k in range(1, size):
        total = total + from_tensor_offset(rows_of(partial_value, (me - k) % size), k, size)
    normed = full_norm(rows_of(residual, me), total, gain)
    pieces = [lax.dynamic_slice_in_dim(normed, me * columns, columns, 1)]
    for k in range(1, size):
        target = (me - k) % size
        pieces.append(
            from_tensor_offset(
                lax.dynamic_slice_in_dim(normed, target * columns, columns, 1), k, size
            )
        )
    ordered = in_device_order(pieces)
    return jnp.concatenate([ordered[j] for j in range(size)], axis=0)


def on_device(
    new_states,
    self_query,
    self_key,
    self_value,
    self_output,
    cross_query,
    cross_output,
    feed_up,
    feed_down,
    norm_self,
    norm_cross,
    norm_feed,
    self_cache,
    cross_cache,
    cache_lengths,
    page_table,
    request_order,
    encoder_lengths,
):
    states = gather_tensor(new_states, 2)
    self_output = gather_tensor(self_output, 0)
    cross_output = gather_tensor(cross_output, 0)
    steps, requests, width = states.shape
    flat = states.reshape(steps * requests, width)
    local_width = self_query.shape[1]
    local_heads = local_width // HEAD_DIM
    scaling = HEAD_DIM ** (-0.5)
    queries = (jnp.dot(flat, self_query, preferred_element_type=jnp.float32) * scaling).astype(
        jnp.bfloat16
    )
    new_keys = jnp.dot(flat, self_key, preferred_element_type=jnp.float32).astype(jnp.bfloat16)
    new_values = jnp.dot(flat, self_value, preferred_element_type=jnp.float32).astype(jnp.bfloat16)
    query_grid = queries.reshape(steps, requests, local_heads, HEAD_DIM)
    key_grid = new_keys.reshape(steps, requests, local_heads, HEAD_DIM)
    value_grid = new_values.reshape(steps, requests, local_heads, HEAD_DIM)
    slot_count = self_cache.shape[0]
    page_width = self_cache.shape[2]
    max_pages = page_table.shape[1]
    seq_index = lax.axis_index("seq")
    seq_size = lax.axis_size("seq")
    flat_table = page_table.reshape(-1)
    entry_ids = jnp.arange(requests * max_pages, dtype=jnp.int32)
    entry_request = entry_ids // max_pages
    entry_page = entry_ids % max_pages
    slot_ids = seq_index * slot_count + jnp.arange(slot_count, dtype=jnp.int32)
    matches = flat_table[None, :] == slot_ids[:, None]
    slot_live = jnp.any(matches, axis=1)
    slot_owner = jnp.sum(jnp.where(matches, entry_request[None, :], 0), axis=1)
    slot_page = jnp.sum(jnp.where(matches, entry_page[None, :], 0), axis=1)
    request_ids = jnp.arange(requests, dtype=jnp.int32)
    slot_length = jnp.sum(
        jnp.where(slot_owner[:, None] == request_ids[None, :], cache_lengths[None, :], 0), axis=1
    )
    positions = slot_page[:, None] * page_width + jnp.arange(page_width, dtype=jnp.int32)[None, :]
    slot_valid = slot_live[:, None] & (positions < slot_length[:, None])
    slot_rows = slot_live[:, None] & (request_order[None, :] == slot_owner[:, None])
    rows_half = slot_rows.astype(jnp.bfloat16)
    rows_wide = slot_rows.astype(jnp.float32)
    slot_query = jnp.einsum(
        "pb,sbc->psc",
        rows_half,
        queries.reshape(steps, requests, local_width),
        preferred_element_type=jnp.float32,
    ).astype(jnp.bfloat16)
    slot_query = slot_query.reshape(slot_count, steps, local_heads, HEAD_DIM)
    cache_keys = self_cache[:, 0].reshape(slot_count, page_width, local_heads, HEAD_DIM)
    cache_values = self_cache[:, 1].reshape(slot_count, page_width, local_heads, HEAD_DIM)
    cache_scores = jnp.einsum(
        "pshd,pkhd->pshk", slot_query, cache_keys, preferred_element_type=jnp.float32
    )
    valid_grid = slot_valid[:, None, None, :]
    slot_max = jnp.max(jnp.where(valid_grid, cache_scores, NEG_FILL), axis=3)
    row_max = jnp.max(
        jnp.where(slot_rows[:, None, :, None], slot_max[:, :, None, :], NEG_FILL), axis=0
    )
    causal = jnp.arange(steps)[None, :] <= jnp.arange(steps)[:, None]
    new_scores = jnp.einsum(
        "tbhd,ubhd->bhtu", query_grid, key_grid, preferred_element_type=jnp.float32
    )
    new_scores = jnp.where(causal, new_scores, NEG_FILL)
    new_max = jnp.transpose(jnp.max(new_scores, axis=3), (2, 0, 1))
    first = seq_index == 0
    local_top = jnp.where(first, jnp.maximum(row_max, new_max), row_max)
    slot_top = jnp.einsum("pb,sbh->psh", rows_wide, local_top, precision=lax.Precision.HIGHEST)
    cache_weights = jnp.exp(jnp.where(valid_grid, cache_scores - slot_top[..., None], NEG_FILL))
    cache_denom = jnp.sum(cache_weights, axis=3)
    cache_numer = jnp.einsum(
        "pshk,pkhd->pshd",
        cache_weights.astype(jnp.bfloat16),
        cache_values,
        preferred_element_type=jnp.float32,
    )
    row_denom = jnp.einsum("pb,psh->sbh", rows_wide, cache_denom, precision=lax.Precision.HIGHEST)
    row_numer = jnp.einsum("pb,pshd->sbhd", rows_wide, cache_numer, precision=lax.Precision.HIGHEST)
    new_top = jnp.maximum(local_top, new_max)
    top_new = jnp.transpose(new_top, (1, 2, 0))[..., None]
    new_weights = jnp.where(causal, jnp.exp(new_scores - top_new), 0.0)
    new_denom = jnp.transpose(jnp.sum(new_weights, axis=3), (2, 0, 1))
    new_numer = jnp.einsum(
        "bhtu,ubhd->tbhd",
        new_weights.astype(jnp.bfloat16),
        value_grid,
        preferred_element_type=jnp.float32,
    )
    row_numer, self_output, cross_output = lax.optimization_barrier(
        (row_numer, self_output, cross_output)
    )
    part_denom = row_denom + jnp.where(first, new_denom, 0.0)
    part_numer = row_numer + jnp.where(first, new_numer, 0.0)
    self_attn = softmax_rows(local_top, part_denom, part_numer, seq_size)
    attn_value = jnp.dot(
        gather_columns(self_attn),
        self_output,
        preferred_element_type=jnp.float32,
    )
    first_full = full_norm(flat, attn_value, norm_self)
    cross_queries = (
        jnp.dot(first_full, cross_query, preferred_element_type=jnp.float32) * scaling
    ).astype(jnp.bfloat16)
    cross_grid = cross_queries.reshape(steps, requests, local_heads, HEAD_DIM)
    order_rows = (request_order[:, None] == request_ids[None, :]).astype(jnp.bfloat16)
    request_query = jnp.einsum(
        "br,sbhd->srhd", order_rows, cross_grid, preferred_element_type=jnp.float32
    ).astype(jnp.bfloat16)
    enc_local = cross_cache.shape[2]
    enc_keys = cross_cache[:, 0].reshape(requests, enc_local, local_heads, HEAD_DIM)
    enc_values = cross_cache[:, 1].reshape(requests, enc_local, local_heads, HEAD_DIM)
    enc_positions = seq_index * enc_local + jnp.arange(enc_local, dtype=jnp.int32)
    enc_valid = (enc_positions[None, :] < encoder_lengths[:, None])[None, :, None, :]
    enc_scores = jnp.einsum(
        "srhd,rehd->srhe", request_query, enc_keys, preferred_element_type=jnp.float32
    )
    enc_local_top = jnp.max(jnp.where(enc_valid, enc_scores, NEG_FILL), axis=3)
    enc_weights = jnp.exp(jnp.where(enc_valid, enc_scores - enc_local_top[..., None], NEG_FILL))
    enc_numer_local = jnp.einsum(
        "srhe,rehd->srhd",
        enc_weights.astype(jnp.bfloat16),
        enc_values,
        preferred_element_type=jnp.float32,
    )
    enc_attn = softmax_rows(
        enc_local_top, jnp.sum(enc_weights, axis=3), enc_numer_local, seq_size
    ).reshape(steps, requests, local_heads, HEAD_DIM)
    cross_attn = jnp.einsum(
        "br,srhd->sbhd", order_rows, enc_attn, preferred_element_type=jnp.float32
    ).astype(jnp.bfloat16)
    attn_value = jnp.dot(
        gather_columns(cross_attn.reshape(steps * requests, local_width)),
        cross_output,
        preferred_element_type=jnp.float32,
    )
    second_full = full_norm(first_full, attn_value, norm_cross)
    ffn_hidden = jax.nn.gelu(
        jnp.dot(second_full, feed_up, preferred_element_type=jnp.float32), approximate=False
    ).astype(jnp.bfloat16)
    out_share = reduce_rows_norm(
        second_full, jnp.dot(ffn_hidden, feed_down, preferred_element_type=jnp.float32), norm_feed
    )
    return out_share.reshape(steps, requests, local_width)


def solution(mesh):
    in_specs = (
        P(None, None, "tensor"),
        P(None, "tensor"),
        P(None, "tensor"),
        P(None, "tensor"),
        P("tensor", None),
        P(None, "tensor"),
        P("tensor", None),
        P(None, "tensor"),
        P("tensor", None),
        P(),
        P(),
        P(),
        P("seq", None, None, "tensor"),
        P(None, None, "seq", "tensor"),
        P(),
        P(),
        P(),
        P(),
    )
    out_specs = P(None, None, "tensor")
    return jax.shard_map(
        on_device, mesh=mesh, in_specs=in_specs, out_specs=out_specs, check_vma=False
    )
```

```python
import jax
import jax.numpy as jnp
from jax import lax
from jax.sharding import PartitionSpec as P

HEAD_DIM = 64


EPSILON = 1e-05
NEG_FILL = -1e30


def layer_norm(summed, gain):
    center = jnp.mean(summed, axis=-1, keepdims=True)
    spread = jnp.mean(summed * summed, axis=-1, keepdims=True) - center * center
    return (summed - center) * lax.rsqrt(spread + EPSILON) * gain


def merge_partials(low, high):
    top_a, denom_a, numer_a = low
    top_b, denom_b, numer_b = high
    top = jnp.maximum(top_a, top_b)
    scale_a = jnp.exp(top_a - top)
    scale_b = jnp.exp(top_b - top)
    denom = denom_a * scale_a + denom_b * scale_b
    numer = numer_a * scale_a[..., None] + numer_b * scale_b[..., None]
    return top, denom, numer


def seq_groups(size):
    groups = []
    distance = 1
    while distance < size:
        width = 4 if distance * 4 <= size else 2
        groups.append((distance, width))
        distance *= width
    return groups


def merge_many(partials):
    top = partials[0][0]
    for other in partials[1:]:
        top = jnp.maximum(top, other[0])
    denom = None
    numer = None
    for part_top, part_denom, part_numer in partials:
        scale = jnp.exp(part_top - top)
        scaled_denom = part_denom * scale
        scaled_numer = part_numer * scale[..., None]
        denom = scaled_denom if denom is None else denom + scaled_denom
        numer = scaled_numer if numer is None else numer + scaled_numer
    return top, denom, numer


def seq_partner(block, offset, size):
    return lax.ppermute(block, "seq", [(i, i ^ offset) for i in range(size)])


def scatter_seq(parts, size):
    index = lax.axis_index("seq")
    for distance, width in seq_groups(size):
        share = parts[0].shape[0] // width
        digit = (index // distance) % width
        partials = [tuple(lax.dynamic_slice_in_dim(x, digit * share, share, 0) for x in parts)]
        for offset in range(1, width):
            target = jnp.bitwise_xor(digit, offset)
            sent = tuple(lax.dynamic_slice_in_dim(x, target * share, share, 0) for x in parts)
            partials.append(seq_partner(sent, offset * distance, size))
        parts = merge_many(partials)
    return parts


def gather_seq(block, size):
    index = lax.axis_index("seq")
    for distance, width in reversed(seq_groups(size)):
        digit = (index // distance) % width
        pieces = [block] + [
            seq_partner(block, offset * distance, size) for offset in range(1, width)
        ]
        order = jnp.bitwise_xor(digit, jnp.arange(width, dtype=digit.dtype))
        block = jnp.take(jnp.stack(pieces), order, axis=0).reshape((-1,) + block.shape[1:])
    return block


def softmax_rows(top, denom, numer, size):
    rows = top.shape[0] * top.shape[1]
    heads = top.shape[2]
    parts = (top.reshape(rows, heads), denom.reshape(rows, heads), numer.reshape(rows, heads, -1))
    top, denom, numer = scatter_seq(parts, size)
    block = (numer / denom[..., None]).astype(jnp.bfloat16)
    return gather_seq(block.reshape(block.shape[0], -1), size)


def full_norm(residual, value, gain):
    return layer_norm(residual.astype(jnp.float32) + value, gain).astype(jnp.bfloat16)


def from_tensor_offset(block, offset, size):
    return lax.ppermute(block, "tensor", [(i, (i - offset) % size) for i in range(size)])


def in_device_order(pieces):
    stacked = jnp.stack(pieces)
    return jnp.roll(stacked, lax.axis_index("tensor"), axis=0)


def gather_tensor(block, axis):
    size = lax.axis_size("tensor")
    pieces = [block] + [from_tensor_offset(block, k, size) for k in range(1, size)]
    ordered = in_device_order(pieces)
    return jnp.concatenate([ordered[j] for j in range(size)], axis=axis)


def gather_columns(block):
    return gather_tensor(block, 1)


def reduce_rows_norm(residual, partial_value, gain):
    size = lax.axis_size("tensor")
    me = lax.axis_index("tensor")
    rows = partial_value.shape[0] // size
    columns = partial_value.shape[1] // size

    def rows_of(value, owner):
        return lax.dynamic_slice_in_dim(value, owner * rows, rows, 0)

    total = rows_of(partial_value, me)
    for k in range(1, size):
        total = total + from_tensor_offset(rows_of(partial_value, (me - k) % size), k, size)
    normed = full_norm(rows_of(residual, me), total, gain)
    pieces = [lax.dynamic_slice_in_dim(normed, me * columns, columns, 1)]
    for k in range(1, size):
        target = (me - k) % size
        pieces.append(
            from_tensor_offset(
                lax.dynamic_slice_in_dim(normed, target * columns, columns, 1), k, size
            )
        )
    ordered = in_device_order(pieces)
    return jnp.concatenate([ordered[j] for j in range(size)], axis=0)


def on_device(
    new_states,
    self_query,
    self_key,
    self_value,
    self_output,
    cross_query,
    cross_output,
    feed_up,
    feed_down,
    norm_self,
    norm_cross,
    norm_feed,
    self_cache,
    cross_cache,
    cache_lengths,
    page_table,
    request_order,
    encoder_lengths,
):
    states = gather_tensor(new_states, 2)
    self_output = gather_tensor(self_output, 0)
    cross_output = gather_tensor(cross_output, 0)
    steps, requests, width = states.shape
    flat = states.reshape(steps * requests, width)
    local_width = self_query.shape[1]
    local_heads = local_width // HEAD_DIM
    scaling = HEAD_DIM ** (-0.5)
    queries = (jnp.dot(flat, self_query, preferred_element_type=jnp.float32) * scaling).astype(
        jnp.bfloat16
    )
    new_keys = jnp.dot(flat, self_key, preferred_element_type=jnp.float32).astype(jnp.bfloat16)
    new_values = jnp.dot(flat, self_value, preferred_element_type=jnp.float32).astype(jnp.bfloat16)
    query_grid = queries.reshape(steps, requests, local_heads, HEAD_DIM)
    key_grid = new_keys.reshape(steps, requests, local_heads, HEAD_DIM)
    value_grid = new_values.reshape(steps, requests, local_heads, HEAD_DIM)
    slot_count = self_cache.shape[0]
    page_width = self_cache.shape[2]
    max_pages = page_table.shape[1]
    seq_index = lax.axis_index("seq")
    seq_size = lax.axis_size("seq")
    flat_table = page_table.reshape(-1)
    entry_ids = jnp.arange(requests * max_pages, dtype=jnp.int32)
    entry_request = entry_ids // max_pages
    entry_page = entry_ids % max_pages
    slot_ids = seq_index * slot_count + jnp.arange(slot_count, dtype=jnp.int32)
    matches = flat_table[None, :] == slot_ids[:, None]
    slot_live = jnp.any(matches, axis=1)
    slot_owner = jnp.sum(jnp.where(matches, entry_request[None, :], 0), axis=1)
    slot_page = jnp.sum(jnp.where(matches, entry_page[None, :], 0), axis=1)
    request_ids = jnp.arange(requests, dtype=jnp.int32)
    slot_length = jnp.sum(
        jnp.where(slot_owner[:, None] == request_ids[None, :], cache_lengths[None, :], 0), axis=1
    )
    positions = slot_page[:, None] * page_width + jnp.arange(page_width, dtype=jnp.int32)[None, :]
    slot_valid = slot_live[:, None] & (positions < slot_length[:, None])
    slot_rows = slot_live[:, None] & (request_order[None, :] == slot_owner[:, None])
    rows_half = slot_rows.astype(jnp.bfloat16)
    rows_wide = slot_rows.astype(jnp.float32)
    slot_query = jnp.einsum(
        "pb,sbc->psc",
        rows_half,
        queries.reshape(steps, requests, local_width),
        preferred_element_type=jnp.float32,
    ).astype(jnp.bfloat16)
    slot_query = slot_query.reshape(slot_count, steps, local_heads, HEAD_DIM)
    cache_keys = self_cache[:, 0].reshape(slot_count, page_width, local_heads, HEAD_DIM)
    cache_values = self_cache[:, 1].reshape(slot_count, page_width, local_heads, HEAD_DIM)
    cache_scores = jnp.einsum(
        "pshd,pkhd->pshk", slot_query, cache_keys, preferred_element_type=jnp.float32
    )
    valid_grid = slot_valid[:, None, None, :]
    slot_max = jnp.max(jnp.where(valid_grid, cache_scores, NEG_FILL), axis=3)
    row_max = jnp.max(
        jnp.where(slot_rows[:, None, :, None], slot_max[:, :, None, :], NEG_FILL), axis=0
    )
    causal = jnp.arange(steps)[None, :] <= jnp.arange(steps)[:, None]
    new_scores = jnp.einsum(
        "tbhd,ubhd->bhtu", query_grid, key_grid, preferred_element_type=jnp.float32
    )
    new_scores = jnp.where(causal, new_scores, NEG_FILL)
    new_max = jnp.transpose(jnp.max(new_scores, axis=3), (2, 0, 1))
    first = seq_index == 0
    local_top = jnp.where(first, jnp.maximum(row_max, new_max), row_max)
    slot_top = jnp.einsum("pb,sbh->psh", rows_wide, local_top, precision=lax.Precision.HIGHEST)
    cache_weights = jnp.exp(jnp.where(valid_grid, cache_scores - slot_top[..., None], NEG_FILL))
    cache_denom = jnp.sum(cache_weights, axis=3)
    cache_numer = jnp.einsum(
        "pshk,pkhd->pshd",
        cache_weights.astype(jnp.bfloat16),
        cache_values,
        preferred_element_type=jnp.float32,
    )
    row_denom = jnp.einsum("pb,psh->sbh", rows_wide, cache_denom, precision=lax.Precision.HIGHEST)
    row_numer = jnp.einsum("pb,pshd->sbhd", rows_wide, cache_numer, precision=lax.Precision.HIGHEST)
    new_top = jnp.maximum(local_top, new_max)
    top_new = jnp.transpose(new_top, (1, 2, 0))[..., None]
    new_weights = jnp.where(causal, jnp.exp(new_scores - top_new), 0.0)
    new_denom = jnp.transpose(jnp.sum(new_weights, axis=3), (2, 0, 1))
    new_numer = jnp.einsum(
        "bhtu,ubhd->tbhd",
        new_weights.astype(jnp.bfloat16),
        value_grid,
        preferred_element_type=jnp.float32,
    )
    part_denom = row_denom + jnp.where(first, new_denom, 0.0)
    part_numer = row_numer + jnp.where(first, new_numer, 0.0)
    self_attn = softmax_rows(local_top, part_denom, part_numer, seq_size)
    attn_value = jnp.dot(
        gather_columns(self_attn),
        self_output,
        preferred_element_type=jnp.float32,
    )
    first_full = full_norm(flat, attn_value, norm_self)
    cross_queries = (
        jnp.dot(first_full, cross_query, preferred_element_type=jnp.float32) * scaling
    ).astype(jnp.bfloat16)
    cross_grid = cross_queries.reshape(steps, requests, local_heads, HEAD_DIM)
    order_rows = (request_order[:, None] == request_ids[None, :]).astype(jnp.bfloat16)
    request_query = jnp.einsum(
        "br,sbhd->srhd", order_rows, cross_grid, preferred_element_type=jnp.float32
    ).astype(jnp.bfloat16)
    enc_local = cross_cache.shape[2]
    enc_keys = cross_cache[:, 0].reshape(requests, enc_local, local_heads, HEAD_DIM)
    enc_values = cross_cache[:, 1].reshape(requests, enc_local, local_heads, HEAD_DIM)
    enc_positions = seq_index * enc_local + jnp.arange(enc_local, dtype=jnp.int32)
    enc_valid = (enc_positions[None, :] < encoder_lengths[:, None])[None, :, None, :]
    enc_scores = jnp.einsum(
        "srhd,rehd->srhe", request_query, enc_keys, preferred_element_type=jnp.float32
    )
    enc_local_top = jnp.max(jnp.where(enc_valid, enc_scores, NEG_FILL), axis=3)
    enc_weights = jnp.exp(jnp.where(enc_valid, enc_scores - enc_local_top[..., None], NEG_FILL))
    enc_numer_local = jnp.einsum(
        "srhe,rehd->srhd",
        enc_weights.astype(jnp.bfloat16),
        enc_values,
        preferred_element_type=jnp.float32,
    )
    enc_attn = softmax_rows(
        enc_local_top, jnp.sum(enc_weights, axis=3), enc_numer_local, seq_size
    ).reshape(steps, requests, local_heads, HEAD_DIM)
    cross_attn = jnp.einsum(
        "br,srhd->sbhd", order_rows, enc_attn, preferred_element_type=jnp.float32
    ).astype(jnp.bfloat16)
    attn_value = jnp.dot(
        gather_columns(cross_attn.reshape(steps * requests, local_width)),
        cross_output,
        preferred_element_type=jnp.float32,
    )
    second_full = full_norm(first_full, attn_value, norm_cross)
    ffn_hidden = jax.nn.gelu(
        jnp.dot(second_full, feed_up, preferred_element_type=jnp.float32), approximate=False
    ).astype(jnp.bfloat16)
    out_share = reduce_rows_norm(
        second_full, jnp.dot(ffn_hidden, feed_down, preferred_element_type=jnp.float32), norm_feed
    )
    return out_share.reshape(steps, requests, local_width)


def solution(mesh):
    in_specs = (
        P(None, None, "tensor"),
        P(None, "tensor"),
        P(None, "tensor"),
        P(None, "tensor"),
        P("tensor", None),
        P(None, "tensor"),
        P("tensor", None),
        P(None, "tensor"),
        P("tensor", None),
        P(),
        P(),
        P(),
        P("seq", None, None, "tensor"),
        P(None, None, "seq", "tensor"),
        P(),
        P(),
        P(),
        P(),
    )
    out_specs = P(None, None, "tensor")
    return jax.shard_map(
        on_device, mesh=mesh, in_specs=in_specs, out_specs=out_specs, check_vma=False
    )
```

```python
import jax
import jax.numpy as jnp
from jax import lax
from jax.sharding import PartitionSpec as P

HEAD_DIM = 64


EPSILON = 1e-05
NEG_FILL = -1e30


def layer_norm(summed, gain):
    center = jnp.mean(summed, axis=-1, keepdims=True)
    spread = jnp.mean(summed * summed, axis=-1, keepdims=True) - center * center
    return (summed - center) * lax.rsqrt(spread + EPSILON) * gain


def merge_partials(low, high):
    stats_a, numer_a = low
    stats_b, numer_b = high
    top = jnp.maximum(stats_a[:, 0], stats_b[:, 0])
    scale_a = jnp.exp(stats_a[:, 0] - top)
    scale_b = jnp.exp(stats_b[:, 0] - top)
    denom = stats_a[:, 1] * scale_a + stats_b[:, 1] * scale_b
    numer = numer_a * scale_a[..., None] + numer_b * scale_b[..., None]
    return jnp.stack([top, denom], axis=1), numer


def scatter_seq(parts, size):
    index = lax.axis_index("seq")
    distance = 1
    while distance < size:
        half = parts[0].shape[0] // 2
        upper = (index & distance) != 0
        keep = jnp.where(upper, half, 0)
        give = half - keep
        mine = tuple(lax.dynamic_slice_in_dim(x, keep, half, 0) for x in parts)
        sent = tuple(lax.dynamic_slice_in_dim(x, give, half, 0) for x in parts)
        theirs = lax.ppermute(sent, "seq", [(i, i ^ distance) for i in range(size)])
        low = tuple(jnp.where(upper, t, m) for m, t in zip(mine, theirs))
        high = tuple(jnp.where(upper, m, t) for m, t in zip(mine, theirs))
        parts = merge_partials(low, high)
        distance *= 2
    return parts


def gather_seq(block, size):
    index = lax.axis_index("seq")
    distance = size // 2
    while distance >= 1:
        theirs = lax.ppermute(block, "seq", [(i, i ^ distance) for i in range(size)])
        upper = (index & distance) != 0
        block = jnp.where(
            upper, jnp.concatenate([theirs, block]), jnp.concatenate([block, theirs])
        )
        distance //= 2
    return block


def softmax_rows(top, denom, numer, size):
    rows = top.shape[0] * top.shape[1]
    heads = top.shape[2]
    stats = jnp.stack([top.reshape(rows, heads), denom.reshape(rows, heads)], axis=1)
    stats, numer = scatter_seq((stats, numer.reshape(rows, heads, -1)), size)
    block = (numer / stats[:, 1][..., None]).astype(jnp.bfloat16)
    return gather_seq(block.reshape(block.shape[0], -1), size)


def full_norm(residual, value, gain):
    return layer_norm(residual.astype(jnp.float32) + value, gain).astype(jnp.bfloat16)


def from_tensor_offset(block, offset, size):
    return lax.ppermute(block, "tensor", [(i, (i - offset) % size) for i in range(size)])


def in_device_order(pieces):
    stacked = jnp.stack(pieces)
    return jnp.roll(stacked, lax.axis_index("tensor"), axis=0)


def gather_tensor(block, axis):
    size = lax.axis_size("tensor")
    pieces = [block] + [from_tensor_offset(block, k, size) for k in range(1, size)]
    ordered = in_device_order(pieces)
    return jnp.concatenate([ordered[j] for j in range(size)], axis=axis)


def gather_columns(block):
    return gather_tensor(block, 1)


def reduce_rows_norm(residual, partial_value, gain):
    size = lax.axis_size("tensor")
    me = lax.axis_index("tensor")
    rows = partial_value.shape[0] // size
    columns = partial_value.shape[1] // size

    def rows_of(value, owner):
        return lax.dynamic_slice_in_dim(value, owner * rows, rows, 0)

    total = rows_of(partial_value, me)
    for k in range(1, size):
        total = total + from_tensor_offset(rows_of(partial_value, (me - k) % size), k, size)
    normed = full_norm(rows_of(residual, me), total, gain)
    pieces = [lax.dynamic_slice_in_dim(normed, me * columns, columns, 1)]
    for k in range(1, size):
        target = (me - k) % size
        pieces.append(
            from_tensor_offset(
                lax.dynamic_slice_in_dim(normed, target * columns, columns, 1), k, size
            )
        )
    ordered = in_device_order(pieces)
    return jnp.concatenate([ordered[j] for j in range(size)], axis=0)


def on_device(
    new_states,
    self_query,
    self_key,
    self_value,
    self_output,
    cross_query,
    cross_output,
    feed_up,
    feed_down,
    norm_self,
    norm_cross,
    norm_feed,
    self_cache,
    cross_cache,
    cache_lengths,
    page_table,
    request_order,
    encoder_lengths,
):
    states = gather_tensor(new_states, 2)
    self_output = gather_tensor(self_output, 0)
    cross_output = gather_tensor(cross_output, 0)
    steps, requests, width = states.shape
    flat = states.reshape(steps * requests, width)
    local_width = self_query.shape[1]
    local_heads = local_width // HEAD_DIM
    scaling = HEAD_DIM ** (-0.5)
    queries = (jnp.dot(flat, self_query, preferred_element_type=jnp.float32) * scaling).astype(
        jnp.bfloat16
    )
    new_keys = jnp.dot(flat, self_key, preferred_element_type=jnp.float32).astype(jnp.bfloat16)
    new_values = jnp.dot(flat, self_value, preferred_element_type=jnp.float32).astype(jnp.bfloat16)
    query_grid = queries.reshape(steps, requests, local_heads, HEAD_DIM)
    key_grid = new_keys.reshape(steps, requests, local_heads, HEAD_DIM)
    value_grid = new_values.reshape(steps, requests, local_heads, HEAD_DIM)
    slot_count = self_cache.shape[0]
    page_width = self_cache.shape[2]
    max_pages = page_table.shape[1]
    seq_index = lax.axis_index("seq")
    seq_size = lax.axis_size("seq")
    flat_table = page_table.reshape(-1)
    entry_ids = jnp.arange(requests * max_pages, dtype=jnp.int32)
    entry_request = entry_ids // max_pages
    entry_page = entry_ids % max_pages
    slot_ids = seq_index * slot_count + jnp.arange(slot_count, dtype=jnp.int32)
    matches = flat_table[None, :] == slot_ids[:, None]
    slot_live = jnp.any(matches, axis=1)
    slot_owner = jnp.sum(jnp.where(matches, entry_request[None, :], 0), axis=1)
    slot_page = jnp.sum(jnp.where(matches, entry_page[None, :], 0), axis=1)
    request_ids = jnp.arange(requests, dtype=jnp.int32)
    slot_length = jnp.sum(
        jnp.where(slot_owner[:, None] == request_ids[None, :], cache_lengths[None, :], 0), axis=1
    )
    positions = slot_page[:, None] * page_width + jnp.arange(page_width, dtype=jnp.int32)[None, :]
    slot_valid = slot_live[:, None] & (positions < slot_length[:, None])
    slot_rows = slot_live[:, None] & (request_order[None, :] == slot_owner[:, None])
    rows_half = slot_rows.astype(jnp.bfloat16)
    rows_wide = slot_rows.astype(jnp.float32)
    slot_query = jnp.einsum(
        "pb,sbc->psc",
        rows_half,
        queries.reshape(steps, requests, local_width),
        preferred_element_type=jnp.float32,
    ).astype(jnp.bfloat16)
    slot_query = slot_query.reshape(slot_count, steps, local_heads, HEAD_DIM)
    cache_keys = self_cache[:, 0].reshape(slot_count, page_width, local_heads, HEAD_DIM)
    cache_values = self_cache[:, 1].reshape(slot_count, page_width, local_heads, HEAD_DIM)
    cache_scores = jnp.einsum(
        "pshd,pkhd->pshk", slot_query, cache_keys, preferred_element_type=jnp.float32
    )
    valid_grid = slot_valid[:, None, None, :]
    slot_max = jnp.max(jnp.where(valid_grid, cache_scores, NEG_FILL), axis=3)
    row_max = jnp.max(
        jnp.where(slot_rows[:, None, :, None], slot_max[:, :, None, :], NEG_FILL), axis=0
    )
    causal = jnp.arange(steps)[None, :] <= jnp.arange(steps)[:, None]
    new_scores = jnp.einsum(
        "tbhd,ubhd->bhtu", query_grid, key_grid, preferred_element_type=jnp.float32
    )
    new_scores = jnp.where(causal, new_scores, NEG_FILL)
    new_max = jnp.transpose(jnp.max(new_scores, axis=3), (2, 0, 1))
    first = seq_index == 0
    local_top = jnp.where(first, jnp.maximum(row_max, new_max), row_max)
    slot_top = jnp.einsum("pb,sbh->psh", rows_wide, local_top, precision=lax.Precision.HIGHEST)
    cache_weights = jnp.exp(jnp.where(valid_grid, cache_scores - slot_top[..., None], NEG_FILL))
    cache_denom = jnp.sum(cache_weights, axis=3)
    cache_numer = jnp.einsum(
        "pshk,pkhd->pshd",
        cache_weights.astype(jnp.bfloat16),
        cache_values,
        preferred_element_type=jnp.float32,
    )
    row_denom = jnp.einsum("pb,psh->sbh", rows_wide, cache_denom, precision=lax.Precision.HIGHEST)
    row_numer = jnp.einsum("pb,pshd->sbhd", rows_wide, cache_numer, precision=lax.Precision.HIGHEST)
    new_top = jnp.maximum(local_top, new_max)
    top_new = jnp.transpose(new_top, (1, 2, 0))[..., None]
    new_weights = jnp.where(causal, jnp.exp(new_scores - top_new), 0.0)
    new_denom = jnp.transpose(jnp.sum(new_weights, axis=3), (2, 0, 1))
    new_numer = jnp.einsum(
        "bhtu,ubhd->tbhd",
        new_weights.astype(jnp.bfloat16),
        value_grid,
        preferred_element_type=jnp.float32,
    )
    part_denom = row_denom + jnp.where(first, new_denom, 0.0)
    part_numer = row_numer + jnp.where(first, new_numer, 0.0)
    self_attn = softmax_rows(local_top, part_denom, part_numer, seq_size)
    attn_value = jnp.dot(
        gather_columns(self_attn),
        self_output,
        preferred_element_type=jnp.float32,
    )
    first_full = full_norm(flat, attn_value, norm_self)
    cross_queries = (
        jnp.dot(first_full, cross_query, preferred_element_type=jnp.float32) * scaling
    ).astype(jnp.bfloat16)
    cross_grid = cross_queries.reshape(steps, requests, local_heads, HEAD_DIM)
    order_rows = (request_order[:, None] == request_ids[None, :]).astype(jnp.bfloat16)
    request_query = jnp.einsum(
        "br,sbhd->srhd", order_rows, cross_grid, preferred_element_type=jnp.float32
    ).astype(jnp.bfloat16)
    enc_local = cross_cache.shape[2]
    enc_keys = cross_cache[:, 0].reshape(requests, enc_local, local_heads, HEAD_DIM)
    enc_values = cross_cache[:, 1].reshape(requests, enc_local, local_heads, HEAD_DIM)
    enc_positions = seq_index * enc_local + jnp.arange(enc_local, dtype=jnp.int32)
    enc_valid = (enc_positions[None, :] < encoder_lengths[:, None])[None, :, None, :]
    enc_scores = jnp.einsum(
        "srhd,rehd->srhe", request_query, enc_keys, preferred_element_type=jnp.float32
    )
    enc_local_top = jnp.max(jnp.where(enc_valid, enc_scores, NEG_FILL), axis=3)
    enc_weights = jnp.exp(jnp.where(enc_valid, enc_scores - enc_local_top[..., None], NEG_FILL))
    enc_numer_local = jnp.einsum(
        "srhe,rehd->srhd",
        enc_weights.astype(jnp.bfloat16),
        enc_values,
        preferred_element_type=jnp.float32,
    )
    enc_attn = softmax_rows(
        enc_local_top, jnp.sum(enc_weights, axis=3), enc_numer_local, seq_size
    ).reshape(steps, requests, local_heads, HEAD_DIM)
    cross_attn = jnp.einsum(
        "br,srhd->sbhd", order_rows, enc_attn, preferred_element_type=jnp.float32
    ).astype(jnp.bfloat16)
    attn_value = jnp.dot(
        gather_columns(cross_attn.reshape(steps * requests, local_width)),
        cross_output,
        preferred_element_type=jnp.float32,
    )
    second_full = full_norm(first_full, attn_value, norm_cross)
    ffn_hidden = jax.nn.gelu(
        jnp.dot(second_full, feed_up, preferred_element_type=jnp.float32), approximate=False
    ).astype(jnp.bfloat16)
    out_share = reduce_rows_norm(
        second_full, jnp.dot(ffn_hidden, feed_down, preferred_element_type=jnp.float32), norm_feed
    )
    return out_share.reshape(steps, requests, local_width)


def solution(mesh):
    in_specs = (
        P(None, None, "tensor"),
        P(None, "tensor"),
        P(None, "tensor"),
        P(None, "tensor"),
        P("tensor", None),
        P(None, "tensor"),
        P("tensor", None),
        P(None, "tensor"),
        P("tensor", None),
        P(),
        P(),
        P(),
        P("seq", None, None, "tensor"),
        P(None, None, "seq", "tensor"),
        P(),
        P(),
        P(),
        P(),
    )
    out_specs = P(None, None, "tensor")
    return jax.shard_map(
        on_device, mesh=mesh, in_specs=in_specs, out_specs=out_specs, check_vma=False
    )
```

```python
import jax
import jax.numpy as jnp
from jax import lax
from jax.sharding import PartitionSpec as P

HEAD_DIM = 64


EPSILON = 1e-05
NEG_FILL = -1e30


def layer_norm(summed, gain):
    center = jnp.mean(summed, axis=-1, keepdims=True)
    spread = jnp.mean(summed * summed, axis=-1, keepdims=True) - center * center
    return (summed - center) * lax.rsqrt(spread + EPSILON) * gain


def merge_partials(low, high):
    stats_a, numer_a = low
    stats_b, numer_b = high
    top = jnp.maximum(stats_a[:, 0], stats_b[:, 0])
    scale_a = jnp.exp(stats_a[:, 0] - top)
    scale_b = jnp.exp(stats_b[:, 0] - top)
    denom = stats_a[:, 1] * scale_a + stats_b[:, 1] * scale_b
    numer = numer_a * scale_a[..., None] + numer_b * scale_b[..., None]
    return jnp.stack([top, denom], axis=1), numer


def scatter_seq(parts, size):
    index = lax.axis_index("seq")
    distance = 1
    while distance < size:
        half = parts[0].shape[0] // 2
        upper = (index & distance) != 0
        keep = jnp.where(upper, half, 0)
        give = half - keep
        mine = tuple(lax.dynamic_slice_in_dim(x, keep, half, 0) for x in parts)
        sent = tuple(lax.dynamic_slice_in_dim(x, give, half, 0) for x in parts)
        theirs = lax.ppermute(sent, "seq", [(i, i ^ distance) for i in range(size)])
        low = tuple(jnp.where(upper, t, m) for m, t in zip(mine, theirs))
        high = tuple(jnp.where(upper, m, t) for m, t in zip(mine, theirs))
        parts = merge_partials(low, high)
        distance *= 2
    return parts


def gather_seq(block, size):
    index = lax.axis_index("seq")
    distance = size // 2
    while distance >= 1:
        theirs = lax.ppermute(block, "seq", [(i, i ^ distance) for i in range(size)])
        upper = (index & distance) != 0
        block = jnp.where(
            upper, jnp.concatenate([theirs, block]), jnp.concatenate([block, theirs])
        )
        distance //= 2
    return block


def softmax_rows(top, denom, numer, size):
    rows = top.shape[0] * top.shape[1]
    heads = top.shape[2]
    stats = jnp.stack([top.reshape(rows, heads), denom.reshape(rows, heads)], axis=1)
    stats, numer = scatter_seq((stats, numer.reshape(rows, heads, -1)), size)
    block = (numer / stats[:, 1][..., None]).astype(jnp.bfloat16)
    return gather_seq(block.reshape(block.shape[0], -1), size)


def full_norm(residual, value, gain):
    return layer_norm(residual.astype(jnp.float32) + value, gain).astype(jnp.bfloat16)


def from_tensor_offset(block, offset, size):
    return lax.ppermute(block, "tensor", [(i, (i - offset) % size) for i in range(size)])


def in_device_order(pieces):
    stacked = jnp.stack(pieces)
    return jnp.roll(stacked, lax.axis_index("tensor"), axis=0)


def gather_tensor(block, axis):
    size = lax.axis_size("tensor")
    pieces = [block] + [from_tensor_offset(block, k, size) for k in range(1, size)]
    ordered = in_device_order(pieces)
    return jnp.concatenate([ordered[j] for j in range(size)], axis=axis)


def gather_columns(block):
    return gather_tensor(block, 1)


def reduce_rows_norm(residual, hidden, weights, gain):
    size = lax.axis_size("tensor")
    me = lax.axis_index("tensor")
    rows = hidden.shape[0] // size
    columns = weights.shape[1] // size

    def rows_of(value, owner):
        return lax.dynamic_slice_in_dim(value, owner * rows, rows, 0)

    def product_rows(owner):
        return jnp.dot(rows_of(hidden, owner), weights, preferred_element_type=jnp.float32)

    arrived = [
        from_tensor_offset(product_rows((me - k) % size), k, size) for k in range(1, size)
    ]
    total = product_rows(me)
    for piece in arrived:
        total = total + piece
    normed = full_norm(rows_of(residual, me), total, gain)
    pieces = [lax.dynamic_slice_in_dim(normed, me * columns, columns, 1)]
    for k in range(1, size):
        target = (me - k) % size
        pieces.append(
            from_tensor_offset(
                lax.dynamic_slice_in_dim(normed, target * columns, columns, 1), k, size
            )
        )
    ordered = in_device_order(pieces)
    return jnp.concatenate([ordered[j] for j in range(size)], axis=0)


def on_device(
    new_states,
    self_query,
    self_key,
    self_value,
    self_output,
    cross_query,
    cross_output,
    feed_up,
    feed_down,
    norm_self,
    norm_cross,
    norm_feed,
    self_cache,
    cross_cache,
    cache_lengths,
    page_table,
    request_order,
    encoder_lengths,
):
    states = gather_tensor(new_states, 2)
    self_output = gather_tensor(self_output, 0)
    cross_output = gather_tensor(cross_output, 0)
    steps, requests, width = states.shape
    flat = states.reshape(steps * requests, width)
    local_width = self_query.shape[1]
    local_heads = local_width // HEAD_DIM
    scaling = HEAD_DIM ** (-0.5)
    queries = (jnp.dot(flat, self_query, preferred_element_type=jnp.float32) * scaling).astype(
        jnp.bfloat16
    )
    new_keys = jnp.dot(flat, self_key, preferred_element_type=jnp.float32).astype(jnp.bfloat16)
    new_values = jnp.dot(flat, self_value, preferred_element_type=jnp.float32).astype(jnp.bfloat16)
    query_grid = queries.reshape(steps, requests, local_heads, HEAD_DIM)
    key_grid = new_keys.reshape(steps, requests, local_heads, HEAD_DIM)
    value_grid = new_values.reshape(steps, requests, local_heads, HEAD_DIM)
    slot_count = self_cache.shape[0]
    page_width = self_cache.shape[2]
    max_pages = page_table.shape[1]
    seq_index = lax.axis_index("seq")
    seq_size = lax.axis_size("seq")
    flat_table = page_table.reshape(-1)
    entry_ids = jnp.arange(requests * max_pages, dtype=jnp.int32)
    entry_request = entry_ids // max_pages
    entry_page = entry_ids % max_pages
    slot_ids = seq_index * slot_count + jnp.arange(slot_count, dtype=jnp.int32)
    matches = flat_table[None, :] == slot_ids[:, None]
    slot_live = jnp.any(matches, axis=1)
    slot_owner = jnp.sum(jnp.where(matches, entry_request[None, :], 0), axis=1)
    slot_page = jnp.sum(jnp.where(matches, entry_page[None, :], 0), axis=1)
    request_ids = jnp.arange(requests, dtype=jnp.int32)
    slot_length = jnp.sum(
        jnp.where(slot_owner[:, None] == request_ids[None, :], cache_lengths[None, :], 0), axis=1
    )
    positions = slot_page[:, None] * page_width + jnp.arange(page_width, dtype=jnp.int32)[None, :]
    slot_valid = slot_live[:, None] & (positions < slot_length[:, None])
    slot_rows = slot_live[:, None] & (request_order[None, :] == slot_owner[:, None])
    rows_half = slot_rows.astype(jnp.bfloat16)
    rows_wide = slot_rows.astype(jnp.float32)
    slot_query = jnp.einsum(
        "pb,sbc->psc",
        rows_half,
        queries.reshape(steps, requests, local_width),
        preferred_element_type=jnp.float32,
    ).astype(jnp.bfloat16)
    slot_query = slot_query.reshape(slot_count, steps, local_heads, HEAD_DIM)
    cache_keys = self_cache[:, 0].reshape(slot_count, page_width, local_heads, HEAD_DIM)
    cache_values = self_cache[:, 1].reshape(slot_count, page_width, local_heads, HEAD_DIM)
    cache_scores = jnp.einsum(
        "pshd,pkhd->pshk", slot_query, cache_keys, preferred_element_type=jnp.float32
    )
    valid_grid = slot_valid[:, None, None, :]
    slot_max = jnp.max(jnp.where(valid_grid, cache_scores, NEG_FILL), axis=3)
    row_max = jnp.max(
        jnp.where(slot_rows[:, None, :, None], slot_max[:, :, None, :], NEG_FILL), axis=0
    )
    causal = jnp.arange(steps)[None, :] <= jnp.arange(steps)[:, None]
    new_scores = jnp.einsum(
        "tbhd,ubhd->bhtu", query_grid, key_grid, preferred_element_type=jnp.float32
    )
    new_scores = jnp.where(causal, new_scores, NEG_FILL)
    new_max = jnp.transpose(jnp.max(new_scores, axis=3), (2, 0, 1))
    first = seq_index == 0
    local_top = jnp.where(first, jnp.maximum(row_max, new_max), row_max)
    slot_top = jnp.einsum("pb,sbh->psh", rows_wide, local_top, precision=lax.Precision.HIGHEST)
    cache_weights = jnp.exp(jnp.where(valid_grid, cache_scores - slot_top[..., None], NEG_FILL))
    cache_denom = jnp.sum(cache_weights, axis=3)
    cache_numer = jnp.einsum(
        "pshk,pkhd->pshd",
        cache_weights.astype(jnp.bfloat16),
        cache_values,
        preferred_element_type=jnp.float32,
    )
    row_denom = jnp.einsum("pb,psh->sbh", rows_wide, cache_denom, precision=lax.Precision.HIGHEST)
    row_numer = jnp.einsum("pb,pshd->sbhd", rows_wide, cache_numer, precision=lax.Precision.HIGHEST)
    new_top = jnp.maximum(local_top, new_max)
    top_new = jnp.transpose(new_top, (1, 2, 0))[..., None]
    new_weights = jnp.where(causal, jnp.exp(new_scores - top_new), 0.0)
    new_denom = jnp.transpose(jnp.sum(new_weights, axis=3), (2, 0, 1))
    new_numer = jnp.einsum(
        "bhtu,ubhd->tbhd",
        new_weights.astype(jnp.bfloat16),
        value_grid,
        preferred_element_type=jnp.float32,
    )
    part_denom = row_denom + jnp.where(first, new_denom, 0.0)
    part_numer = row_numer + jnp.where(first, new_numer, 0.0)
    self_attn = softmax_rows(local_top, part_denom, part_numer, seq_size)
    attn_value = jnp.dot(
        gather_columns(self_attn),
        self_output,
        preferred_element_type=jnp.float32,
    )
    first_full = full_norm(flat, attn_value, norm_self)
    cross_queries = (
        jnp.dot(first_full, cross_query, preferred_element_type=jnp.float32) * scaling
    ).astype(jnp.bfloat16)
    cross_grid = cross_queries.reshape(steps, requests, local_heads, HEAD_DIM)
    order_rows = (request_order[:, None] == request_ids[None, :]).astype(jnp.bfloat16)
    request_query = jnp.einsum(
        "br,sbhd->srhd", order_rows, cross_grid, preferred_element_type=jnp.float32
    ).astype(jnp.bfloat16)
    enc_local = cross_cache.shape[2]
    enc_keys = cross_cache[:, 0].reshape(requests, enc_local, local_heads, HEAD_DIM)
    enc_values = cross_cache[:, 1].reshape(requests, enc_local, local_heads, HEAD_DIM)
    enc_positions = seq_index * enc_local + jnp.arange(enc_local, dtype=jnp.int32)
    enc_valid = (enc_positions[None, :] < encoder_lengths[:, None])[None, :, None, :]
    enc_scores = jnp.einsum(
        "srhd,rehd->srhe", request_query, enc_keys, preferred_element_type=jnp.float32
    )
    enc_local_top = jnp.max(jnp.where(enc_valid, enc_scores, NEG_FILL), axis=3)
    enc_weights = jnp.exp(jnp.where(enc_valid, enc_scores - enc_local_top[..., None], NEG_FILL))
    enc_numer_local = jnp.einsum(
        "srhe,rehd->srhd",
        enc_weights.astype(jnp.bfloat16),
        enc_values,
        preferred_element_type=jnp.float32,
    )
    enc_attn = softmax_rows(
        enc_local_top, jnp.sum(enc_weights, axis=3), enc_numer_local, seq_size
    ).reshape(steps, requests, local_heads, HEAD_DIM)
    cross_attn = jnp.einsum(
        "br,srhd->sbhd", order_rows, enc_attn, preferred_element_type=jnp.float32
    ).astype(jnp.bfloat16)
    attn_value = jnp.dot(
        gather_columns(cross_attn.reshape(steps * requests, local_width)),
        cross_output,
        preferred_element_type=jnp.float32,
    )
    second_full = full_norm(first_full, attn_value, norm_cross)
    ffn_hidden = jax.nn.gelu(
        jnp.dot(second_full, feed_up, preferred_element_type=jnp.float32), approximate=False
    ).astype(jnp.bfloat16)
    out_share = reduce_rows_norm(second_full, ffn_hidden, feed_down, norm_feed)
    return out_share.reshape(steps, requests, local_width)


def solution(mesh):
    in_specs = (
        P(None, None, "tensor"),
        P(None, "tensor"),
        P(None, "tensor"),
        P(None, "tensor"),
        P("tensor", None),
        P(None, "tensor"),
        P("tensor", None),
        P(None, "tensor"),
        P("tensor", None),
        P(),
        P(),
        P(),
        P("seq", None, None, "tensor"),
        P(None, None, "seq", "tensor"),
        P(),
        P(),
        P(),
        P(),
    )
    out_specs = P(None, None, "tensor")
    return jax.shard_map(
        on_device, mesh=mesh, in_specs=in_specs, out_specs=out_specs, check_vma=False
    )
```

```python
import jax
import jax.numpy as jnp
from jax import lax
from jax.sharding import PartitionSpec as P

HEAD_DIM = 64


EPSILON = 1e-05
NEG_FILL = -1e30


def layer_norm(summed, gain):
    center = jnp.mean(summed, axis=-1, keepdims=True)
    spread = jnp.mean(summed * summed, axis=-1, keepdims=True) - center * center
    return (summed - center) * lax.rsqrt(spread + EPSILON) * gain


def merge_partials(low, high):
    stats_a, numer_a = low
    stats_b, numer_b = high
    top = jnp.maximum(stats_a[:, 0], stats_b[:, 0])
    scale_a = jnp.exp(stats_a[:, 0] - top)
    scale_b = jnp.exp(stats_b[:, 0] - top)
    denom = stats_a[:, 1] * scale_a + stats_b[:, 1] * scale_b
    numer = numer_a * scale_a[..., None] + numer_b * scale_b[..., None]
    return jnp.stack([top, denom], axis=1), numer


def scatter_seq(parts, size, held=()):
    index = lax.axis_index("seq")
    distance = 1
    while distance < size:
        if distance * distance == size or (distance * distance * 2 == size):
            parts, held = lax.optimization_barrier((parts, held))
        half = parts[0].shape[0] // 2
        upper = (index & distance) != 0
        keep = jnp.where(upper, half, 0)
        give = half - keep
        mine = tuple(lax.dynamic_slice_in_dim(x, keep, half, 0) for x in parts)
        sent = tuple(lax.dynamic_slice_in_dim(x, give, half, 0) for x in parts)
        theirs = lax.ppermute(sent, "seq", [(i, i ^ distance) for i in range(size)])
        low = tuple(jnp.where(upper, t, m) for m, t in zip(mine, theirs))
        high = tuple(jnp.where(upper, m, t) for m, t in zip(mine, theirs))
        parts = merge_partials(low, high)
        distance *= 2
    return parts, held


def gather_seq(block, size):
    index = lax.axis_index("seq")
    distance = size // 2
    while distance >= 1:
        theirs = lax.ppermute(block, "seq", [(i, i ^ distance) for i in range(size)])
        upper = (index & distance) != 0
        block = jnp.where(
            upper, jnp.concatenate([theirs, block]), jnp.concatenate([block, theirs])
        )
        distance //= 2
    return block


def softmax_rows(top, denom, numer, size, held=()):
    rows = top.shape[0] * top.shape[1]
    heads = top.shape[2]
    stats = jnp.stack([top.reshape(rows, heads), denom.reshape(rows, heads)], axis=1)
    (stats, numer), held = scatter_seq((stats, numer.reshape(rows, heads, -1)), size, held)
    block = (numer / stats[:, 1][..., None]).astype(jnp.bfloat16)
    return gather_seq(block.reshape(block.shape[0], -1), size), held


def full_norm(residual, value, gain):
    return layer_norm(residual.astype(jnp.float32) + value, gain).astype(jnp.bfloat16)


def from_tensor_offset(block, offset, size):
    return lax.ppermute(block, "tensor", [(i, (i - offset) % size) for i in range(size)])


def in_device_order(pieces):
    stacked = jnp.stack(pieces)
    return jnp.roll(stacked, lax.axis_index("tensor"), axis=0)


def gather_tensor(block, axis):
    size = lax.axis_size("tensor")
    pieces = [block] + [from_tensor_offset(block, k, size) for k in range(1, size)]
    ordered = in_device_order(pieces)
    return jnp.concatenate([ordered[j] for j in range(size)], axis=axis)


def gather_columns(block):
    return gather_tensor(block, 1)


def reduce_rows_norm(residual, hidden, weights, gain):
    size = lax.axis_size("tensor")
    me = lax.axis_index("tensor")
    rows = hidden.shape[0] // size
    columns = weights.shape[1] // size

    def rows_of(value, owner):
        return lax.dynamic_slice_in_dim(value, owner * rows, rows, 0)

    def product_rows(owner):
        return jnp.dot(rows_of(hidden, owner), weights, preferred_element_type=jnp.float32)

    arrived = [
        from_tensor_offset(product_rows((me - k) % size), k, size) for k in range(1, size)
    ]
    total = product_rows(me)
    for piece in arrived:
        total = total + piece
    normed = full_norm(rows_of(residual, me), total, gain)
    pieces = [lax.dynamic_slice_in_dim(normed, me * columns, columns, 1)]
    for k in range(1, size):
        target = (me - k) % size
        pieces.append(
            from_tensor_offset(
                lax.dynamic_slice_in_dim(normed, target * columns, columns, 1), k, size
            )
        )
    ordered = in_device_order(pieces)
    return jnp.concatenate([ordered[j] for j in range(size)], axis=0)


def on_device(
    new_states,
    self_query,
    self_key,
    self_value,
    self_output,
    cross_query,
    cross_output,
    feed_up,
    feed_down,
    norm_self,
    norm_cross,
    norm_feed,
    self_cache,
    cross_cache,
    cache_lengths,
    page_table,
    request_order,
    encoder_lengths,
):
    states = gather_tensor(new_states, 2)
    self_output = gather_tensor(self_output, 0)
    cross_output = gather_tensor(cross_output, 0)
    steps, requests, width = states.shape
    flat = states.reshape(steps * requests, width)
    local_width = self_query.shape[1]
    local_heads = local_width // HEAD_DIM
    scaling = HEAD_DIM ** (-0.5)
    queries = (jnp.dot(flat, self_query, preferred_element_type=jnp.float32) * scaling).astype(
        jnp.bfloat16
    )
    new_keys = jnp.dot(flat, self_key, preferred_element_type=jnp.float32).astype(jnp.bfloat16)
    new_values = jnp.dot(flat, self_value, preferred_element_type=jnp.float32).astype(jnp.bfloat16)
    query_grid = queries.reshape(steps, requests, local_heads, HEAD_DIM)
    key_grid = new_keys.reshape(steps, requests, local_heads, HEAD_DIM)
    value_grid = new_values.reshape(steps, requests, local_heads, HEAD_DIM)
    slot_count = self_cache.shape[0]
    page_width = self_cache.shape[2]
    max_pages = page_table.shape[1]
    seq_index = lax.axis_index("seq")
    seq_size = lax.axis_size("seq")
    flat_table = page_table.reshape(-1)
    entry_ids = jnp.arange(requests * max_pages, dtype=jnp.int32)
    entry_request = entry_ids // max_pages
    entry_page = entry_ids % max_pages
    slot_ids = seq_index * slot_count + jnp.arange(slot_count, dtype=jnp.int32)
    matches = flat_table[None, :] == slot_ids[:, None]
    slot_live = jnp.any(matches, axis=1)
    slot_owner = jnp.sum(jnp.where(matches, entry_request[None, :], 0), axis=1)
    slot_page = jnp.sum(jnp.where(matches, entry_page[None, :], 0), axis=1)
    request_ids = jnp.arange(requests, dtype=jnp.int32)
    slot_length = jnp.sum(
        jnp.where(slot_owner[:, None] == request_ids[None, :], cache_lengths[None, :], 0), axis=1
    )
    positions = slot_page[:, None] * page_width + jnp.arange(page_width, dtype=jnp.int32)[None, :]
    slot_valid = slot_live[:, None] & (positions < slot_length[:, None])
    slot_rows = slot_live[:, None] & (request_order[None, :] == slot_owner[:, None])
    rows_half = slot_rows.astype(jnp.bfloat16)
    rows_wide = slot_rows.astype(jnp.float32)
    slot_query = jnp.einsum(
        "pb,sbc->psc",
        rows_half,
        queries.reshape(steps, requests, local_width),
        preferred_element_type=jnp.float32,
    ).astype(jnp.bfloat16)
    slot_query = slot_query.reshape(slot_count, steps, local_heads, HEAD_DIM)
    cache_keys = self_cache[:, 0].reshape(slot_count, page_width, local_heads, HEAD_DIM)
    cache_values = self_cache[:, 1].reshape(slot_count, page_width, local_heads, HEAD_DIM)
    cache_scores = jnp.einsum(
        "pshd,pkhd->pshk", slot_query, cache_keys, preferred_element_type=jnp.float32
    )
    valid_grid = slot_valid[:, None, None, :]
    slot_max = jnp.max(jnp.where(valid_grid, cache_scores, NEG_FILL), axis=3)
    row_max = jnp.max(
        jnp.where(slot_rows[:, None, :, None], slot_max[:, :, None, :], NEG_FILL), axis=0
    )
    causal = jnp.arange(steps)[None, :] <= jnp.arange(steps)[:, None]
    new_scores = jnp.einsum(
        "tbhd,ubhd->bhtu", query_grid, key_grid, preferred_element_type=jnp.float32
    )
    new_scores = jnp.where(causal, new_scores, NEG_FILL)
    new_max = jnp.transpose(jnp.max(new_scores, axis=3), (2, 0, 1))
    first = seq_index == 0
    local_top = jnp.where(first, jnp.maximum(row_max, new_max), row_max)
    slot_top = jnp.einsum("pb,sbh->psh", rows_wide, local_top, precision=lax.Precision.HIGHEST)
    cache_weights = jnp.exp(jnp.where(valid_grid, cache_scores - slot_top[..., None], NEG_FILL))
    cache_denom = jnp.sum(cache_weights, axis=3)
    cache_numer = jnp.einsum(
        "pshk,pkhd->pshd",
        cache_weights.astype(jnp.bfloat16),
        cache_values,
        preferred_element_type=jnp.float32,
    )
    row_denom = jnp.einsum("pb,psh->sbh", rows_wide, cache_denom, precision=lax.Precision.HIGHEST)
    row_numer = jnp.einsum("pb,pshd->sbhd", rows_wide, cache_numer, precision=lax.Precision.HIGHEST)
    new_top = jnp.maximum(local_top, new_max)
    top_new = jnp.transpose(new_top, (1, 2, 0))[..., None]
    new_weights = jnp.where(causal, jnp.exp(new_scores - top_new), 0.0)
    new_denom = jnp.transpose(jnp.sum(new_weights, axis=3), (2, 0, 1))
    new_numer = jnp.einsum(
        "bhtu,ubhd->tbhd",
        new_weights.astype(jnp.bfloat16),
        value_grid,
        preferred_element_type=jnp.float32,
    )
    part_denom = row_denom + jnp.where(first, new_denom, 0.0)
    part_numer = row_numer + jnp.where(first, new_numer, 0.0)
    self_attn, (self_output, cross_output) = softmax_rows(
        local_top, part_denom, part_numer, seq_size, (self_output, cross_output)
    )
    attn_value = jnp.dot(
        gather_columns(self_attn),
        self_output,
        preferred_element_type=jnp.float32,
    )
    first_full = full_norm(flat, attn_value, norm_self)
    cross_queries = (
        jnp.dot(first_full, cross_query, preferred_element_type=jnp.float32) * scaling
    ).astype(jnp.bfloat16)
    cross_grid = cross_queries.reshape(steps, requests, local_heads, HEAD_DIM)
    order_rows = (request_order[:, None] == request_ids[None, :]).astype(jnp.bfloat16)
    request_query = jnp.einsum(
        "br,sbhd->srhd", order_rows, cross_grid, preferred_element_type=jnp.float32
    ).astype(jnp.bfloat16)
    enc_local = cross_cache.shape[2]
    enc_keys = cross_cache[:, 0].reshape(requests, enc_local, local_heads, HEAD_DIM)
    enc_values = cross_cache[:, 1].reshape(requests, enc_local, local_heads, HEAD_DIM)
    enc_positions = seq_index * enc_local + jnp.arange(enc_local, dtype=jnp.int32)
    enc_valid = (enc_positions[None, :] < encoder_lengths[:, None])[None, :, None, :]
    enc_scores = jnp.einsum(
        "srhd,rehd->srhe", request_query, enc_keys, preferred_element_type=jnp.float32
    )
    enc_local_top = jnp.max(jnp.where(enc_valid, enc_scores, NEG_FILL), axis=3)
    enc_weights = jnp.exp(jnp.where(enc_valid, enc_scores - enc_local_top[..., None], NEG_FILL))
    enc_numer_local = jnp.einsum(
        "srhe,rehd->srhd",
        enc_weights.astype(jnp.bfloat16),
        enc_values,
        preferred_element_type=jnp.float32,
    )
    enc_attn = softmax_rows(
        enc_local_top, jnp.sum(enc_weights, axis=3), enc_numer_local, seq_size
    )[0].reshape(steps, requests, local_heads, HEAD_DIM)
    cross_attn = jnp.einsum(
        "br,srhd->sbhd", order_rows, enc_attn, preferred_element_type=jnp.float32
    ).astype(jnp.bfloat16)
    attn_value = jnp.dot(
        gather_columns(cross_attn.reshape(steps * requests, local_width)),
        cross_output,
        preferred_element_type=jnp.float32,
    )
    second_full = full_norm(first_full, attn_value, norm_cross)
    ffn_hidden = jax.nn.gelu(
        jnp.dot(second_full, feed_up, preferred_element_type=jnp.float32), approximate=False
    ).astype(jnp.bfloat16)
    out_share = reduce_rows_norm(second_full, ffn_hidden, feed_down, norm_feed)
    return out_share.reshape(steps, requests, local_width)


def solution(mesh):
    in_specs = (
        P(None, None, "tensor"),
        P(None, "tensor"),
        P(None, "tensor"),
        P(None, "tensor"),
        P("tensor", None),
        P(None, "tensor"),
        P("tensor", None),
        P(None, "tensor"),
        P("tensor", None),
        P(),
        P(),
        P(),
        P("seq", None, None, "tensor"),
        P(None, None, "seq", "tensor"),
        P(),
        P(),
        P(),
        P(),
    )
    out_specs = P(None, None, "tensor")
    return jax.shard_map(
        on_device, mesh=mesh, in_specs=in_specs, out_specs=out_specs, check_vma=False
    )
```

```python
import jax
import jax.numpy as jnp
from jax import lax
from jax.sharding import PartitionSpec as P

HEAD_DIM = 64


EPSILON = 1e-05
NEG_FILL = -1e30


def layer_norm(summed, gain):
    center = jnp.mean(summed, axis=-1, keepdims=True)
    spread = jnp.mean(summed * summed, axis=-1, keepdims=True) - center * center
    return (summed - center) * lax.rsqrt(spread + EPSILON) * gain


def merge_partials(low, high):
    stats_a, numer_a = low
    stats_b, numer_b = high
    top = jnp.maximum(stats_a[:, 0], stats_b[:, 0])
    scale_a = jnp.exp(stats_a[:, 0] - top)
    scale_b = jnp.exp(stats_b[:, 0] - top)
    denom = stats_a[:, 1] * scale_a + stats_b[:, 1] * scale_b
    numer = numer_a * scale_a[..., None] + numer_b * scale_b[..., None]
    return jnp.stack([top, denom], axis=1), numer


def scatter_seq(parts, size):
    index = lax.axis_index("seq")
    distance = 1
    while distance < size:
        half = parts[0].shape[0] // 2
        upper = (index & distance) != 0
        keep = jnp.where(upper, half, 0)
        give = half - keep
        mine = tuple(lax.dynamic_slice_in_dim(x, keep, half, 0) for x in parts)
        sent = tuple(lax.dynamic_slice_in_dim(x, give, half, 0) for x in parts)
        theirs = lax.ppermute(sent, "seq", [(i, i ^ distance) for i in range(size)])
        low = tuple(jnp.where(upper, t, m) for m, t in zip(mine, theirs))
        high = tuple(jnp.where(upper, m, t) for m, t in zip(mine, theirs))
        parts = merge_partials(low, high)
        distance *= 2
    return parts


def gather_seq(block, size):
    index = lax.axis_index("seq")
    distance = size // 2
    while distance >= 1:
        theirs = lax.ppermute(block, "seq", [(i, i ^ distance) for i in range(size)])
        upper = (index & distance) != 0
        block = jnp.where(
            upper, jnp.concatenate([theirs, block]), jnp.concatenate([block, theirs])
        )
        distance //= 2
    return block


def softmax_rows(top, denom, numer, size):
    rows = top.shape[0] * top.shape[1]
    heads = top.shape[2]
    stats = jnp.stack([top.reshape(rows, heads), denom.reshape(rows, heads)], axis=1)
    stats, numer = scatter_seq((stats, numer.reshape(rows, heads, -1)), size)
    block = (numer / stats[:, 1][..., None]).astype(jnp.bfloat16)
    return gather_seq(block.reshape(block.shape[0], -1), size)


def full_norm(residual, value, gain):
    return layer_norm(residual.astype(jnp.float32) + value, gain).astype(jnp.bfloat16)


def from_tensor_offset(block, offset, size):
    return lax.ppermute(block, "tensor", [(i, (i - offset) % size) for i in range(size)])


def in_device_order(pieces):
    stacked = jnp.stack(pieces)
    return jnp.roll(stacked, lax.axis_index("tensor"), axis=0)


def gather_tensor(block, axis):
    size = lax.axis_size("tensor")
    pieces = [block] + [from_tensor_offset(block, k, size) for k in range(1, size)]
    ordered = in_device_order(pieces)
    return jnp.concatenate([ordered[j] for j in range(size)], axis=axis)


def gather_columns(block):
    return gather_tensor(block, 1)


def reduce_rows_norm(residual, product_of, gain):
    size = lax.axis_size("tensor")
    me = lax.axis_index("tensor")
    rows = residual.shape[0] // size
    columns = residual.shape[1] // size

    def rows_of(value, owner):
        return lax.dynamic_slice_in_dim(value, owner * rows, rows, 0)

    def product_rows(owner):
        return product_of(rows_of(residual, owner))

    arrived = [
        from_tensor_offset(product_rows((me - k) % size), k, size) for k in range(1, size)
    ]
    total = product_rows(me)
    for piece in arrived:
        total = total + piece
    normed = full_norm(rows_of(residual, me), total, gain)
    pieces = [lax.dynamic_slice_in_dim(normed, me * columns, columns, 1)]
    for k in range(1, size):
        target = (me - k) % size
        pieces.append(
            from_tensor_offset(
                lax.dynamic_slice_in_dim(normed, target * columns, columns, 1), k, size
            )
        )
    ordered = in_device_order(pieces)
    return jnp.concatenate([ordered[j] for j in range(size)], axis=0)


def on_device(
    new_states,
    self_query,
    self_key,
    self_value,
    self_output,
    cross_query,
    cross_output,
    feed_up,
    feed_down,
    norm_self,
    norm_cross,
    norm_feed,
    self_cache,
    cross_cache,
    cache_lengths,
    page_table,
    request_order,
    encoder_lengths,
):
    states = gather_tensor(new_states, 2)
    self_output = gather_tensor(self_output, 0)
    cross_output = gather_tensor(cross_output, 0)
    steps, requests, width = states.shape
    flat = states.reshape(steps * requests, width)
    local_width = self_query.shape[1]
    local_heads = local_width // HEAD_DIM
    scaling = HEAD_DIM ** (-0.5)
    queries = (jnp.dot(flat, self_query, preferred_element_type=jnp.float32) * scaling).astype(
        jnp.bfloat16
    )
    new_keys = jnp.dot(flat, self_key, preferred_element_type=jnp.float32).astype(jnp.bfloat16)
    new_values = jnp.dot(flat, self_value, preferred_element_type=jnp.float32).astype(jnp.bfloat16)
    query_grid = queries.reshape(steps, requests, local_heads, HEAD_DIM)
    key_grid = new_keys.reshape(steps, requests, local_heads, HEAD_DIM)
    value_grid = new_values.reshape(steps, requests, local_heads, HEAD_DIM)
    slot_count = self_cache.shape[0]
    page_width = self_cache.shape[2]
    max_pages = page_table.shape[1]
    seq_index = lax.axis_index("seq")
    seq_size = lax.axis_size("seq")
    flat_table = page_table.reshape(-1)
    entry_ids = jnp.arange(requests * max_pages, dtype=jnp.int32)
    entry_request = entry_ids // max_pages
    entry_page = entry_ids % max_pages
    slot_ids = seq_index * slot_count + jnp.arange(slot_count, dtype=jnp.int32)
    matches = flat_table[None, :] == slot_ids[:, None]
    slot_live = jnp.any(matches, axis=1)
    slot_owner = jnp.sum(jnp.where(matches, entry_request[None, :], 0), axis=1)
    slot_page = jnp.sum(jnp.where(matches, entry_page[None, :], 0), axis=1)
    request_ids = jnp.arange(requests, dtype=jnp.int32)
    slot_length = jnp.sum(
        jnp.where(slot_owner[:, None] == request_ids[None, :], cache_lengths[None, :], 0), axis=1
    )
    positions = slot_page[:, None] * page_width + jnp.arange(page_width, dtype=jnp.int32)[None, :]
    slot_valid = slot_live[:, None] & (positions < slot_length[:, None])
    slot_rows = slot_live[:, None] & (request_order[None, :] == slot_owner[:, None])
    rows_half = slot_rows.astype(jnp.bfloat16)
    rows_wide = slot_rows.astype(jnp.float32)
    slot_query = jnp.einsum(
        "pb,sbc->psc",
        rows_half,
        queries.reshape(steps, requests, local_width),
        preferred_element_type=jnp.float32,
    ).astype(jnp.bfloat16)
    slot_query = slot_query.reshape(slot_count, steps, local_heads, HEAD_DIM)
    cache_keys = self_cache[:, 0].reshape(slot_count, page_width, local_heads, HEAD_DIM)
    cache_values = self_cache[:, 1].reshape(slot_count, page_width, local_heads, HEAD_DIM)
    cache_scores = jnp.einsum(
        "pshd,pkhd->pshk", slot_query, cache_keys, preferred_element_type=jnp.float32
    )
    valid_grid = slot_valid[:, None, None, :]
    slot_max = jnp.max(jnp.where(valid_grid, cache_scores, NEG_FILL), axis=3)
    row_max = jnp.max(
        jnp.where(slot_rows[:, None, :, None], slot_max[:, :, None, :], NEG_FILL), axis=0
    )
    causal = jnp.arange(steps)[None, :] <= jnp.arange(steps)[:, None]
    new_scores = jnp.einsum(
        "tbhd,ubhd->bhtu", query_grid, key_grid, preferred_element_type=jnp.float32
    )
    new_scores = jnp.where(causal, new_scores, NEG_FILL)
    new_max = jnp.transpose(jnp.max(new_scores, axis=3), (2, 0, 1))
    first = seq_index == 0
    local_top = jnp.where(first, jnp.maximum(row_max, new_max), row_max)
    slot_top = jnp.einsum("pb,sbh->psh", rows_wide, local_top, precision=lax.Precision.HIGHEST)
    cache_weights = jnp.exp(jnp.where(valid_grid, cache_scores - slot_top[..., None], NEG_FILL))
    cache_denom = jnp.sum(cache_weights, axis=3)
    cache_numer = jnp.einsum(
        "pshk,pkhd->pshd",
        cache_weights.astype(jnp.bfloat16),
        cache_values,
        preferred_element_type=jnp.float32,
    )
    row_denom = jnp.einsum("pb,psh->sbh", rows_wide, cache_denom, precision=lax.Precision.HIGHEST)
    row_numer = jnp.einsum("pb,pshd->sbhd", rows_wide, cache_numer, precision=lax.Precision.HIGHEST)
    new_top = jnp.maximum(local_top, new_max)
    top_new = jnp.transpose(new_top, (1, 2, 0))[..., None]
    new_weights = jnp.where(causal, jnp.exp(new_scores - top_new), 0.0)
    new_denom = jnp.transpose(jnp.sum(new_weights, axis=3), (2, 0, 1))
    new_numer = jnp.einsum(
        "bhtu,ubhd->tbhd",
        new_weights.astype(jnp.bfloat16),
        value_grid,
        preferred_element_type=jnp.float32,
    )
    part_denom = row_denom + jnp.where(first, new_denom, 0.0)
    part_numer = row_numer + jnp.where(first, new_numer, 0.0)
    self_attn = softmax_rows(local_top, part_denom, part_numer, seq_size)
    attn_value = jnp.dot(
        gather_columns(self_attn),
        self_output,
        preferred_element_type=jnp.float32,
    )
    first_full = full_norm(flat, attn_value, norm_self)
    cross_queries = (
        jnp.dot(first_full, cross_query, preferred_element_type=jnp.float32) * scaling
    ).astype(jnp.bfloat16)
    cross_grid = cross_queries.reshape(steps, requests, local_heads, HEAD_DIM)
    order_rows = (request_order[:, None] == request_ids[None, :]).astype(jnp.bfloat16)
    request_query = jnp.einsum(
        "br,sbhd->srhd", order_rows, cross_grid, preferred_element_type=jnp.float32
    ).astype(jnp.bfloat16)
    enc_local = cross_cache.shape[2]
    enc_keys = cross_cache[:, 0].reshape(requests, enc_local, local_heads, HEAD_DIM)
    enc_values = cross_cache[:, 1].reshape(requests, enc_local, local_heads, HEAD_DIM)
    enc_positions = seq_index * enc_local + jnp.arange(enc_local, dtype=jnp.int32)
    enc_valid = (enc_positions[None, :] < encoder_lengths[:, None])[None, :, None, :]
    enc_scores = jnp.einsum(
        "srhd,rehd->srhe", request_query, enc_keys, preferred_element_type=jnp.float32
    )
    enc_local_top = jnp.max(jnp.where(enc_valid, enc_scores, NEG_FILL), axis=3)
    enc_weights = jnp.exp(jnp.where(enc_valid, enc_scores - enc_local_top[..., None], NEG_FILL))
    enc_numer_local = jnp.einsum(
        "srhe,rehd->srhd",
        enc_weights.astype(jnp.bfloat16),
        enc_values,
        preferred_element_type=jnp.float32,
    )
    enc_attn = softmax_rows(
        enc_local_top, jnp.sum(enc_weights, axis=3), enc_numer_local, seq_size
    ).reshape(steps, requests, local_heads, HEAD_DIM)
    cross_attn = jnp.einsum(
        "br,srhd->sbhd", order_rows, enc_attn, preferred_element_type=jnp.float32
    ).astype(jnp.bfloat16)
    attn_value = jnp.dot(
        gather_columns(cross_attn.reshape(steps * requests, local_width)),
        cross_output,
        preferred_element_type=jnp.float32,
    )
    second_full = full_norm(first_full, attn_value, norm_cross)

    def feed_forward(rows):
        ffn_hidden = jax.nn.gelu(
            jnp.dot(rows, feed_up, preferred_element_type=jnp.float32), approximate=False
        ).astype(jnp.bfloat16)
        return jnp.dot(ffn_hidden, feed_down, preferred_element_type=jnp.float32)

    out_share = reduce_rows_norm(second_full, feed_forward, norm_feed)
    return out_share.reshape(steps, requests, local_width)


def solution(mesh):
    in_specs = (
        P(None, None, "tensor"),
        P(None, "tensor"),
        P(None, "tensor"),
        P(None, "tensor"),
        P("tensor", None),
        P(None, "tensor"),
        P("tensor", None),
        P(None, "tensor"),
        P("tensor", None),
        P(),
        P(),
        P(),
        P("seq", None, None, "tensor"),
        P(None, None, "seq", "tensor"),
        P(),
        P(),
        P(),
        P(),
    )
    out_specs = P(None, None, "tensor")
    return jax.shard_map(
        on_device, mesh=mesh, in_specs=in_specs, out_specs=out_specs, check_vma=False
    )
```

```python
import jax
import jax.numpy as jnp
from jax import lax
from jax.sharding import PartitionSpec as P

HEAD_DIM = 64


EPSILON = 1e-05
NEG_FILL = -1e30


def layer_norm(summed, gain):
    center = jnp.mean(summed, axis=-1, keepdims=True)
    spread = jnp.mean(summed * summed, axis=-1, keepdims=True) - center * center
    return (summed - center) * lax.rsqrt(spread + EPSILON) * gain


def merge_partials(low, high):
    stats_a, numer_a = low
    stats_b, numer_b = high
    top = jnp.maximum(stats_a[:, 0], stats_b[:, 0])
    scale_a = jnp.exp(stats_a[:, 0] - top)
    scale_b = jnp.exp(stats_b[:, 0] - top)
    denom = stats_a[:, 1] * scale_a + stats_b[:, 1] * scale_b
    numer = numer_a * scale_a[..., None] + numer_b * scale_b[..., None]
    return jnp.stack([top, denom], axis=1), numer


def scatter_seq(parts, size):
    index = lax.axis_index("seq")
    distance = 1
    while distance < size:
        half = parts[0].shape[0] // 2
        upper = (index & distance) != 0
        keep = jnp.where(upper, half, 0)
        give = half - keep
        mine = tuple(lax.dynamic_slice_in_dim(x, keep, half, 0) for x in parts)
        sent = tuple(lax.dynamic_slice_in_dim(x, give, half, 0) for x in parts)
        theirs = lax.ppermute(sent, "seq", [(i, i ^ distance) for i in range(size)])
        low = tuple(jnp.where(upper, t, m) for m, t in zip(mine, theirs))
        high = tuple(jnp.where(upper, m, t) for m, t in zip(mine, theirs))
        parts = merge_partials(low, high)
        distance *= 2
    return parts


def gather_seq(block, size):
    index = lax.axis_index("seq")
    distance = size // 2
    while distance >= 1:
        theirs = lax.ppermute(block, "seq", [(i, i ^ distance) for i in range(size)])
        upper = (index & distance) != 0
        block = jnp.where(
            upper, jnp.concatenate([theirs, block]), jnp.concatenate([block, theirs])
        )
        distance //= 2
    return block


def softmax_rows(top, denom, numer, size):
    rows = top.shape[0] * top.shape[1]
    heads = top.shape[2]
    stats = jnp.stack([top.reshape(rows, heads), denom.reshape(rows, heads)], axis=1)
    stats, numer = scatter_seq((stats, numer.reshape(rows, heads, -1)), size)
    block = (numer / stats[:, 1][..., None]).astype(jnp.bfloat16)
    return gather_seq(block.reshape(block.shape[0], -1), size)


def full_norm(residual, value, gain):
    return layer_norm(residual.astype(jnp.float32) + value, gain).astype(jnp.bfloat16)


def from_tensor_offset(block, offset, size):
    return lax.ppermute(block, "tensor", [(i, (i - offset) % size) for i in range(size)])


def in_device_order(pieces):
    stacked = jnp.stack(pieces)
    return jnp.roll(stacked, lax.axis_index("tensor"), axis=0)


def gather_tensor(block, axis):
    size = lax.axis_size("tensor")
    pieces = [block] + [from_tensor_offset(block, k, size) for k in range(1, size)]
    ordered = in_device_order(pieces)
    return jnp.concatenate([ordered[j] for j in range(size)], axis=axis)


def gather_columns(block):
    return gather_tensor(block, 1)


def reduce_columns_norm(residual, hidden, weights, gain):
    size = lax.axis_size("tensor")
    me = lax.axis_index("tensor")
    columns = weights.shape[1] // size

    def columns_of(value, owner):
        return lax.dynamic_slice_in_dim(value, owner * columns, columns, value.ndim - 1)

    def product_columns(owner):
        return jnp.dot(hidden, columns_of(weights, owner), preferred_element_type=jnp.float32)

    arrived = [
        from_tensor_offset(product_columns((me - k) % size), k, size) for k in range(1, size)
    ]
    total = product_columns(me)
    for piece in arrived:
        total = total + piece
    summed = columns_of(residual, me).astype(jnp.float32) + total
    part = jnp.stack([jnp.sum(summed, axis=-1), jnp.sum(summed * summed, axis=-1)], axis=1)
    stats = part
    for k in range(1, size):
        stats = stats + from_tensor_offset(part, k, size)
    width = residual.shape[1]
    center = stats[:, 0:1] / width
    spread = stats[:, 1:2] / width - center * center
    normed = (summed - center) * lax.rsqrt(spread + EPSILON) * columns_of(gain, me)
    return normed.astype(jnp.bfloat16)


def on_device(
    new_states,
    self_query,
    self_key,
    self_value,
    self_output,
    cross_query,
    cross_output,
    feed_up,
    feed_down,
    norm_self,
    norm_cross,
    norm_feed,
    self_cache,
    cross_cache,
    cache_lengths,
    page_table,
    request_order,
    encoder_lengths,
):
    states = gather_tensor(new_states, 2)
    self_output = gather_tensor(self_output, 0)
    cross_output = gather_tensor(cross_output, 0)
    steps, requests, width = states.shape
    flat = states.reshape(steps * requests, width)
    local_width = self_query.shape[1]
    local_heads = local_width // HEAD_DIM
    scaling = HEAD_DIM ** (-0.5)
    queries = (jnp.dot(flat, self_query, preferred_element_type=jnp.float32) * scaling).astype(
        jnp.bfloat16
    )
    new_keys = jnp.dot(flat, self_key, preferred_element_type=jnp.float32).astype(jnp.bfloat16)
    new_values = jnp.dot(flat, self_value, preferred_element_type=jnp.float32).astype(jnp.bfloat16)
    query_grid = queries.reshape(steps, requests, local_heads, HEAD_DIM)
    key_grid = new_keys.reshape(steps, requests, local_heads, HEAD_DIM)
    value_grid = new_values.reshape(steps, requests, local_heads, HEAD_DIM)
    slot_count = self_cache.shape[0]
    page_width = self_cache.shape[2]
    max_pages = page_table.shape[1]
    seq_index = lax.axis_index("seq")
    seq_size = lax.axis_size("seq")
    flat_table = page_table.reshape(-1)
    entry_ids = jnp.arange(requests * max_pages, dtype=jnp.int32)
    entry_request = entry_ids // max_pages
    entry_page = entry_ids % max_pages
    slot_ids = seq_index * slot_count + jnp.arange(slot_count, dtype=jnp.int32)
    matches = flat_table[None, :] == slot_ids[:, None]
    slot_live = jnp.any(matches, axis=1)
    slot_owner = jnp.sum(jnp.where(matches, entry_request[None, :], 0), axis=1)
    slot_page = jnp.sum(jnp.where(matches, entry_page[None, :], 0), axis=1)
    request_ids = jnp.arange(requests, dtype=jnp.int32)
    slot_length = jnp.sum(
        jnp.where(slot_owner[:, None] == request_ids[None, :], cache_lengths[None, :], 0), axis=1
    )
    positions = slot_page[:, None] * page_width + jnp.arange(page_width, dtype=jnp.int32)[None, :]
    slot_valid = slot_live[:, None] & (positions < slot_length[:, None])
    slot_rows = slot_live[:, None] & (request_order[None, :] == slot_owner[:, None])
    rows_half = slot_rows.astype(jnp.bfloat16)
    rows_wide = slot_rows.astype(jnp.float32)
    slot_query = jnp.einsum(
        "pb,sbc->psc",
        rows_half,
        queries.reshape(steps, requests, local_width),
        preferred_element_type=jnp.float32,
    ).astype(jnp.bfloat16)
    slot_query = slot_query.reshape(slot_count, steps, local_heads, HEAD_DIM)
    cache_keys = self_cache[:, 0].reshape(slot_count, page_width, local_heads, HEAD_DIM)
    cache_values = self_cache[:, 1].reshape(slot_count, page_width, local_heads, HEAD_DIM)
    cache_scores = jnp.einsum(
        "pshd,pkhd->pshk", slot_query, cache_keys, preferred_element_type=jnp.float32
    )
    valid_grid = slot_valid[:, None, None, :]
    slot_max = jnp.max(jnp.where(valid_grid, cache_scores, NEG_FILL), axis=3)
    row_max = jnp.max(
        jnp.where(slot_rows[:, None, :, None], slot_max[:, :, None, :], NEG_FILL), axis=0
    )
    causal = jnp.arange(steps)[None, :] <= jnp.arange(steps)[:, None]
    new_scores = jnp.einsum(
        "tbhd,ubhd->bhtu", query_grid, key_grid, preferred_element_type=jnp.float32
    )
    new_scores = jnp.where(causal, new_scores, NEG_FILL)
    new_max = jnp.transpose(jnp.max(new_scores, axis=3), (2, 0, 1))
    first = seq_index == 0
    local_top = jnp.where(first, jnp.maximum(row_max, new_max), row_max)
    slot_top = jnp.einsum("pb,sbh->psh", rows_wide, local_top, precision=lax.Precision.HIGHEST)
    cache_weights = jnp.exp(jnp.where(valid_grid, cache_scores - slot_top[..., None], NEG_FILL))
    cache_denom = jnp.sum(cache_weights, axis=3)
    cache_numer = jnp.einsum(
        "pshk,pkhd->pshd",
        cache_weights.astype(jnp.bfloat16),
        cache_values,
        preferred_element_type=jnp.float32,
    )
    row_denom = jnp.einsum("pb,psh->sbh", rows_wide, cache_denom, precision=lax.Precision.HIGHEST)
    row_numer = jnp.einsum("pb,pshd->sbhd", rows_wide, cache_numer, precision=lax.Precision.HIGHEST)
    new_top = jnp.maximum(local_top, new_max)
    top_new = jnp.transpose(new_top, (1, 2, 0))[..., None]
    new_weights = jnp.where(causal, jnp.exp(new_scores - top_new), 0.0)
    new_denom = jnp.transpose(jnp.sum(new_weights, axis=3), (2, 0, 1))
    new_numer = jnp.einsum(
        "bhtu,ubhd->tbhd",
        new_weights.astype(jnp.bfloat16),
        value_grid,
        preferred_element_type=jnp.float32,
    )
    part_denom = row_denom + jnp.where(first, new_denom, 0.0)
    part_numer = row_numer + jnp.where(first, new_numer, 0.0)
    self_attn = softmax_rows(local_top, part_denom, part_numer, seq_size)
    attn_value = jnp.dot(
        gather_columns(self_attn),
        self_output,
        preferred_element_type=jnp.float32,
    )
    first_full = full_norm(flat, attn_value, norm_self)
    cross_queries = (
        jnp.dot(first_full, cross_query, preferred_element_type=jnp.float32) * scaling
    ).astype(jnp.bfloat16)
    cross_grid = cross_queries.reshape(steps, requests, local_heads, HEAD_DIM)
    order_rows = (request_order[:, None] == request_ids[None, :]).astype(jnp.bfloat16)
    request_query = jnp.einsum(
        "br,sbhd->srhd", order_rows, cross_grid, preferred_element_type=jnp.float32
    ).astype(jnp.bfloat16)
    enc_local = cross_cache.shape[2]
    enc_keys = cross_cache[:, 0].reshape(requests, enc_local, local_heads, HEAD_DIM)
    enc_values = cross_cache[:, 1].reshape(requests, enc_local, local_heads, HEAD_DIM)
    enc_positions = seq_index * enc_local + jnp.arange(enc_local, dtype=jnp.int32)
    enc_valid = (enc_positions[None, :] < encoder_lengths[:, None])[None, :, None, :]
    enc_scores = jnp.einsum(
        "srhd,rehd->srhe", request_query, enc_keys, preferred_element_type=jnp.float32
    )
    enc_local_top = jnp.max(jnp.where(enc_valid, enc_scores, NEG_FILL), axis=3)
    enc_weights = jnp.exp(jnp.where(enc_valid, enc_scores - enc_local_top[..., None], NEG_FILL))
    enc_numer_local = jnp.einsum(
        "srhe,rehd->srhd",
        enc_weights.astype(jnp.bfloat16),
        enc_values,
        preferred_element_type=jnp.float32,
    )
    enc_attn = softmax_rows(
        enc_local_top, jnp.sum(enc_weights, axis=3), enc_numer_local, seq_size
    ).reshape(steps, requests, local_heads, HEAD_DIM)
    cross_attn = jnp.einsum(
        "br,srhd->sbhd", order_rows, enc_attn, preferred_element_type=jnp.float32
    ).astype(jnp.bfloat16)
    attn_value = jnp.dot(
        gather_columns(cross_attn.reshape(steps * requests, local_width)),
        cross_output,
        preferred_element_type=jnp.float32,
    )
    second_full = full_norm(first_full, attn_value, norm_cross)
    ffn_hidden = jax.nn.gelu(
        jnp.dot(second_full, feed_up, preferred_element_type=jnp.float32), approximate=False
    ).astype(jnp.bfloat16)
    out_share = reduce_columns_norm(second_full, ffn_hidden, feed_down, norm_feed)
    return out_share.reshape(steps, requests, local_width)


def solution(mesh):
    in_specs = (
        P(None, None, "tensor"),
        P(None, "tensor"),
        P(None, "tensor"),
        P(None, "tensor"),
        P("tensor", None),
        P(None, "tensor"),
        P("tensor", None),
        P(None, "tensor"),
        P("tensor", None),
        P(),
        P(),
        P(),
        P("seq", None, None, "tensor"),
        P(None, None, "seq", "tensor"),
        P(),
        P(),
        P(),
        P(),
    )
    out_specs = P(None, None, "tensor")
    return jax.shard_map(
        on_device, mesh=mesh, in_specs=in_specs, out_specs=out_specs, check_vma=False
    )
```

```python
import jax
import jax.numpy as jnp
from jax import lax
from jax.sharding import PartitionSpec as P

HEAD_DIM = 64


EPSILON = 1e-05
NEG_FILL = -1e30


def layer_norm(summed, gain):
    center = jnp.mean(summed, axis=-1, keepdims=True)
    spread = jnp.mean(summed * summed, axis=-1, keepdims=True) - center * center
    return (summed - center) * lax.rsqrt(spread + EPSILON) * gain


def merge_partials(low, high):
    stats_a, numer_a = low
    stats_b, numer_b = high
    top = jnp.maximum(stats_a[:, 0], stats_b[:, 0])
    scale_a = jnp.exp(stats_a[:, 0] - top)
    scale_b = jnp.exp(stats_b[:, 0] - top)
    denom = stats_a[:, 1] * scale_a + stats_b[:, 1] * scale_b
    numer = numer_a * scale_a[..., None] + numer_b * scale_b[..., None]
    return jnp.stack([top, denom], axis=1), numer


def scatter_seq(parts, size, held=()):
    index = lax.axis_index("seq")
    distance = 1
    while distance < size:
        if distance * distance == size or distance * distance * 2 == size:
            parts, held = lax.optimization_barrier((parts, held))
        half = parts[0].shape[0] // 2
        upper = (index & distance) != 0
        keep = jnp.where(upper, half, 0)
        give = half - keep
        mine = tuple(lax.dynamic_slice_in_dim(x, keep, half, 0) for x in parts)
        sent = tuple(lax.dynamic_slice_in_dim(x, give, half, 0) for x in parts)
        theirs = lax.ppermute(sent, "seq", [(i, i ^ distance) for i in range(size)])
        low = tuple(jnp.where(upper, t, m) for m, t in zip(mine, theirs))
        high = tuple(jnp.where(upper, m, t) for m, t in zip(mine, theirs))
        parts = merge_partials(low, high)
        distance *= 2
    return parts, held


def gather_seq(block, size):
    index = lax.axis_index("seq")
    distance = size // 2
    while distance >= 1:
        theirs = lax.ppermute(block, "seq", [(i, i ^ distance) for i in range(size)])
        upper = (index & distance) != 0
        block = jnp.where(
            upper, jnp.concatenate([theirs, block]), jnp.concatenate([block, theirs])
        )
        distance //= 2
    return block


def softmax_rows(top, denom, numer, size, held=()):
    rows = top.shape[0] * top.shape[1]
    heads = top.shape[2]
    stats = jnp.stack([top.reshape(rows, heads), denom.reshape(rows, heads)], axis=1)
    (stats, numer), held = scatter_seq((stats, numer.reshape(rows, heads, -1)), size, held)
    block = (numer / stats[:, 1][..., None]).astype(jnp.bfloat16)
    return gather_seq(block.reshape(block.shape[0], -1), size), held


def full_norm(residual, value, gain):
    return layer_norm(residual.astype(jnp.float32) + value, gain).astype(jnp.bfloat16)


def from_tensor_offset(block, offset, size):
    return lax.ppermute(block, "tensor", [(i, (i - offset) % size) for i in range(size)])


def in_device_order(pieces):
    stacked = jnp.stack(pieces)
    return jnp.roll(stacked, lax.axis_index("tensor"), axis=0)


def gather_tensor(block, axis):
    size = lax.axis_size("tensor")
    pieces = [block] + [from_tensor_offset(block, k, size) for k in range(1, size)]
    ordered = in_device_order(pieces)
    return jnp.concatenate([ordered[j] for j in range(size)], axis=axis)


def gather_columns(block):
    return gather_tensor(block, 1)


def reduce_columns_norm(residual, hidden, weights, gain):
    size = lax.axis_size("tensor")
    me = lax.axis_index("tensor")
    columns = weights.shape[1] // size

    def columns_of(value, owner):
        return lax.dynamic_slice_in_dim(value, owner * columns, columns, value.ndim - 1)

    def product_columns(owner):
        return jnp.dot(hidden, columns_of(weights, owner), preferred_element_type=jnp.float32)

    arrived = [
        from_tensor_offset(product_columns((me - k) % size), k, size) for k in range(1, size)
    ]
    total = product_columns(me)
    for piece in arrived:
        total = total + piece
    summed = columns_of(residual, me).astype(jnp.float32) + total
    part = jnp.stack([jnp.sum(summed, axis=-1), jnp.sum(summed * summed, axis=-1)], axis=1)
    stats = part
    for k in range(1, size):
        stats = stats + from_tensor_offset(part, k, size)
    width = residual.shape[1]
    center = stats[:, 0:1] / width
    spread = stats[:, 1:2] / width - center * center
    normed = (summed - center) * lax.rsqrt(spread + EPSILON) * columns_of(gain, me)
    return normed.astype(jnp.bfloat16)


def on_device(
    new_states,
    self_query,
    self_key,
    self_value,
    self_output,
    cross_query,
    cross_output,
    feed_up,
    feed_down,
    norm_self,
    norm_cross,
    norm_feed,
    self_cache,
    cross_cache,
    cache_lengths,
    page_table,
    request_order,
    encoder_lengths,
):
    states = gather_tensor(new_states, 2)
    self_output = gather_tensor(self_output, 0)
    cross_output = gather_tensor(cross_output, 0)
    steps, requests, width = states.shape
    flat = states.reshape(steps * requests, width)
    local_width = self_query.shape[1]
    local_heads = local_width // HEAD_DIM
    scaling = HEAD_DIM ** (-0.5)
    queries = (jnp.dot(flat, self_query, preferred_element_type=jnp.float32) * scaling).astype(
        jnp.bfloat16
    )
    new_keys = jnp.dot(flat, self_key, preferred_element_type=jnp.float32).astype(jnp.bfloat16)
    new_values = jnp.dot(flat, self_value, preferred_element_type=jnp.float32).astype(jnp.bfloat16)
    query_grid = queries.reshape(steps, requests, local_heads, HEAD_DIM)
    key_grid = new_keys.reshape(steps, requests, local_heads, HEAD_DIM)
    value_grid = new_values.reshape(steps, requests, local_heads, HEAD_DIM)
    slot_count = self_cache.shape[0]
    page_width = self_cache.shape[2]
    max_pages = page_table.shape[1]
    seq_index = lax.axis_index("seq")
    seq_size = lax.axis_size("seq")
    flat_table = page_table.reshape(-1)
    entry_ids = jnp.arange(requests * max_pages, dtype=jnp.int32)
    entry_request = entry_ids // max_pages
    entry_page = entry_ids % max_pages
    slot_ids = seq_index * slot_count + jnp.arange(slot_count, dtype=jnp.int32)
    matches = flat_table[None, :] == slot_ids[:, None]
    slot_live = jnp.any(matches, axis=1)
    slot_owner = jnp.sum(jnp.where(matches, entry_request[None, :], 0), axis=1)
    slot_page = jnp.sum(jnp.where(matches, entry_page[None, :], 0), axis=1)
    request_ids = jnp.arange(requests, dtype=jnp.int32)
    slot_length = jnp.sum(
        jnp.where(slot_owner[:, None] == request_ids[None, :], cache_lengths[None, :], 0), axis=1
    )
    positions = slot_page[:, None] * page_width + jnp.arange(page_width, dtype=jnp.int32)[None, :]
    slot_valid = slot_live[:, None] & (positions < slot_length[:, None])
    slot_rows = slot_live[:, None] & (request_order[None, :] == slot_owner[:, None])
    rows_half = slot_rows.astype(jnp.bfloat16)
    rows_wide = slot_rows.astype(jnp.float32)
    slot_query = jnp.einsum(
        "pb,sbc->psc",
        rows_half,
        queries.reshape(steps, requests, local_width),
        preferred_element_type=jnp.float32,
    ).astype(jnp.bfloat16)
    slot_query = slot_query.reshape(slot_count, steps, local_heads, HEAD_DIM)
    cache_keys = self_cache[:, 0].reshape(slot_count, page_width, local_heads, HEAD_DIM)
    cache_values = self_cache[:, 1].reshape(slot_count, page_width, local_heads, HEAD_DIM)
    cache_scores = jnp.einsum(
        "pshd,pkhd->pshk", slot_query, cache_keys, preferred_element_type=jnp.float32
    )
    valid_grid = slot_valid[:, None, None, :]
    slot_max = jnp.max(jnp.where(valid_grid, cache_scores, NEG_FILL), axis=3)
    row_max = jnp.max(
        jnp.where(slot_rows[:, None, :, None], slot_max[:, :, None, :], NEG_FILL), axis=0
    )
    causal = jnp.arange(steps)[None, :] <= jnp.arange(steps)[:, None]
    new_scores = jnp.einsum(
        "tbhd,ubhd->bhtu", query_grid, key_grid, preferred_element_type=jnp.float32
    )
    new_scores = jnp.where(causal, new_scores, NEG_FILL)
    new_max = jnp.transpose(jnp.max(new_scores, axis=3), (2, 0, 1))
    first = seq_index == 0
    local_top = jnp.where(first, jnp.maximum(row_max, new_max), row_max)
    slot_top = jnp.einsum("pb,sbh->psh", rows_wide, local_top, precision=lax.Precision.HIGHEST)
    cache_weights = jnp.exp(jnp.where(valid_grid, cache_scores - slot_top[..., None], NEG_FILL))
    cache_denom = jnp.sum(cache_weights, axis=3)
    cache_numer = jnp.einsum(
        "pshk,pkhd->pshd",
        cache_weights.astype(jnp.bfloat16),
        cache_values,
        preferred_element_type=jnp.float32,
    )
    row_denom = jnp.einsum("pb,psh->sbh", rows_wide, cache_denom, precision=lax.Precision.HIGHEST)
    row_numer = jnp.einsum("pb,pshd->sbhd", rows_wide, cache_numer, precision=lax.Precision.HIGHEST)
    new_top = jnp.maximum(local_top, new_max)
    top_new = jnp.transpose(new_top, (1, 2, 0))[..., None]
    new_weights = jnp.where(causal, jnp.exp(new_scores - top_new), 0.0)
    new_denom = jnp.transpose(jnp.sum(new_weights, axis=3), (2, 0, 1))
    new_numer = jnp.einsum(
        "bhtu,ubhd->tbhd",
        new_weights.astype(jnp.bfloat16),
        value_grid,
        preferred_element_type=jnp.float32,
    )
    part_denom = row_denom + jnp.where(first, new_denom, 0.0)
    part_numer = row_numer + jnp.where(first, new_numer, 0.0)
    self_attn = softmax_rows(local_top, part_denom, part_numer, seq_size)[0]
    attn_value = jnp.dot(
        gather_columns(self_attn),
        self_output,
        preferred_element_type=jnp.float32,
    )
    first_full = full_norm(flat, attn_value, norm_self)
    cross_queries = (
        jnp.dot(first_full, cross_query, preferred_element_type=jnp.float32) * scaling
    ).astype(jnp.bfloat16)
    cross_grid = cross_queries.reshape(steps, requests, local_heads, HEAD_DIM)
    order_rows = (request_order[:, None] == request_ids[None, :]).astype(jnp.bfloat16)
    request_query = jnp.einsum(
        "br,sbhd->srhd", order_rows, cross_grid, preferred_element_type=jnp.float32
    ).astype(jnp.bfloat16)
    enc_local = cross_cache.shape[2]
    enc_keys = cross_cache[:, 0].reshape(requests, enc_local, local_heads, HEAD_DIM)
    enc_values = cross_cache[:, 1].reshape(requests, enc_local, local_heads, HEAD_DIM)
    enc_positions = seq_index * enc_local + jnp.arange(enc_local, dtype=jnp.int32)
    enc_valid = (enc_positions[None, :] < encoder_lengths[:, None])[None, :, None, :]
    enc_scores = jnp.einsum(
        "srhd,rehd->srhe", request_query, enc_keys, preferred_element_type=jnp.float32
    )
    enc_local_top = jnp.max(jnp.where(enc_valid, enc_scores, NEG_FILL), axis=3)
    enc_weights = jnp.exp(jnp.where(enc_valid, enc_scores - enc_local_top[..., None], NEG_FILL))
    enc_numer_local = jnp.einsum(
        "srhe,rehd->srhd",
        enc_weights.astype(jnp.bfloat16),
        enc_values,
        preferred_element_type=jnp.float32,
    )
    enc_attn, cross_output = softmax_rows(
        enc_local_top, jnp.sum(enc_weights, axis=3), enc_numer_local, seq_size, cross_output
    )
    enc_attn = enc_attn.reshape(steps, requests, local_heads, HEAD_DIM)
    cross_attn = jnp.einsum(
        "br,srhd->sbhd", order_rows, enc_attn, preferred_element_type=jnp.float32
    ).astype(jnp.bfloat16)
    attn_value = jnp.dot(
        gather_columns(cross_attn.reshape(steps * requests, local_width)),
        cross_output,
        preferred_element_type=jnp.float32,
    )
    second_full = full_norm(first_full, attn_value, norm_cross)
    ffn_hidden = jax.nn.gelu(
        jnp.dot(second_full, feed_up, preferred_element_type=jnp.float32), approximate=False
    ).astype(jnp.bfloat16)
    out_share = reduce_columns_norm(second_full, ffn_hidden, feed_down, norm_feed)
    return out_share.reshape(steps, requests, local_width)


def solution(mesh):
    in_specs = (
        P(None, None, "tensor"),
        P(None, "tensor"),
        P(None, "tensor"),
        P(None, "tensor"),
        P("tensor", None),
        P(None, "tensor"),
        P("tensor", None),
        P(None, "tensor"),
        P("tensor", None),
        P(),
        P(),
        P(),
        P("seq", None, None, "tensor"),
        P(None, None, "seq", "tensor"),
        P(),
        P(),
        P(),
        P(),
    )
    out_specs = P(None, None, "tensor")
    return jax.shard_map(
        on_device, mesh=mesh, in_specs=in_specs, out_specs=out_specs, check_vma=False
    )
```
